512 devices in a mesh: req: 128 (over y, z, core), tp: 4 (over x).
Axes of the slice: x: 4, y: 8, z: 8, core: 2. Of those that a mesh axis runs over, the one named last changes fastest.
Arguments:
- tokens: bfloat16 [32768, 2048], P('req', 'tp'), may hold values from -18 to 18
- gain: float32 [2048], replicated, may hold values from 0.25 to 1.75
- qkv_weight: bfloat16 [3, 2048, 1024], P(None, None, 'tp'), may hold values from -1 to 1
- adapter_in: bfloat16 [128, 2048, 32], P('req', 'tp'), may hold values from -0.125 to 0.125
- adapter_out: bfloat16 [128, 2, 16, 1024], P('req', None, None, 'tp'), may hold values from -0.75 to 0.75
- request_of: int32 [128, 256], P('req'), may hold values from 0 to 16, as said below
- adapter_of: int32 [128, 16], P('req'), may hold values from 0 to 127, as said below
- block_row: int32 [128, 256], P('req'), may hold values from 0 to 15, as said below
Outputs:
- context: bfloat16 [32768, 1024], P('req', 'tp')
The draws below stay inside these ranges and needn't reach their ends.
Inputs may be any that keep to these rules, and one draw needn't show every extreme that they name: `request_of`: the rows of a group are its requests 0 to 15 in order of index, each of at most 16 rows, then padding rows marked 16; requests whose index is a multiple of 128 have exactly 16 rows. `adapter_of`: requests of one group whose indices differ by a multiple of 128 share an adapter, other requests of the group have different adapters; so at most 16 live rows of a group use one adapter, and in every draw some adapter gets exactly 16 live rows from every group. `block_row`: for a live row, the number of earlier live rows of its group with the same adapter; 0 on padding rows.
All inputs are finite; a program needn't handle non-finite values.
Results may differ from the reference program's by a relative error of at most 0.0095.
Values may be sent and summed in bfloat16 or wider, within the bound.
No kernel may reach another device: no remote copies, remote signals or barrier semaphores. Data moves between devices by JAX's collectives and lax.ppermute only.
A program may use at most 64 MiB of HBM per device.

```python
import jax
import jax.numpy as jnp
from jax import lax

D = 2048
HEADS = 16
HEAD = 64
RANK = 16
LMAX = 16
TOK_DEV = 256
GROUPS = 128
ADAPTERS = 128
CAP = 16
SLOTS = 2048
TOKENS = 32768


def arrangement(key):
    base = jax.random.fold_in(key, 41)
    k_len, k_pop, k_top, k_pick = jax.random.split(base, 4)
    count = TOK_DEV // LMAX
    index = jnp.arange(count, dtype=jnp.int32)
    request_lengths = jax.random.randint(k_len, (GROUPS, count), LMAX // 2, LMAX + 1, dtype=jnp.int32)
    request_lengths = jnp.where((index % ADAPTERS == 0)[None, :], LMAX, request_lengths).astype(jnp.int32)
    ends = jnp.cumsum(request_lengths, axis=1).astype(jnp.int32)
    starts = ends - request_lengths
    position = jnp.arange(TOK_DEV, dtype=jnp.int32)
    request_entry = jnp.sum((ends[:, None, :] <= position[None, :, None]).astype(jnp.int32), axis=2).astype(jnp.int32)
    labels = jnp.arange(ADAPTERS, dtype=jnp.int32)
    popular = jax.random.randint(k_pop, (ADAPTERS,), 0, 4096, dtype=jnp.int32)
    leader = jax.random.randint(k_top, (), 0, ADAPTERS, dtype=jnp.int32)
    score = jax.random.randint(k_pick, (GROUPS, ADAPTERS), 0, 4096, dtype=jnp.int32) + 2 * popular[None, :]
    score = score + jnp.where(labels == leader, 1 << 20, 0).astype(jnp.int32)[None, :]
    order = lax.top_k(score * ADAPTERS + labels[None, :], ADAPTERS)[1].astype(jnp.int32)
    picks = jnp.broadcast_to(index % ADAPTERS, (GROUPS, count)).astype(jnp.int32)
    adapter = jnp.take_along_axis(order, picks, axis=1).astype(jnp.int32)
    same = (index[:, None] % ADAPTERS == index[None, :] % ADAPTERS) & (index[None, :] < index[:, None])
    before = jnp.sum(jnp.where(same[None, :, :], request_lengths[:, None, :], 0), axis=2).astype(jnp.int32)
    clipped = jnp.minimum(request_entry, count - 1).astype(jnp.int32)
    row = jnp.take_along_axis(before, clipped, axis=1) + position[None, :] - jnp.take_along_axis(starts, clipped, axis=1)
    row = jnp.where(request_entry < count, row, 0).astype(jnp.int32)
    return (request_entry, adapter, row)


def draw_request_of(key, part):
    return arrangement(key)[0]


def draw_adapter_of(key, part):
    return arrangement(key)[1]


def draw_block_row(key, part):
    return arrangement(key)[2]


def draw_tokens(key, part):
    k_base = jax.random.fold_in(jax.random.fold_in(key, 3), 0)
    base = jnp.clip(jax.random.normal(k_base, (TOKENS, D), jnp.float32), -6.0, 6.0)
    values = base
    return values.astype(jnp.bfloat16)


def draw_qkv_weight(key, part):
    k_base = jax.random.fold_in(jax.random.fold_in(key, 5), 0)
    base = jnp.clip(jax.random.normal(k_base, (3, D, HEADS * HEAD), jnp.float32), -6.0, 6.0) * D ** (-0.5)
    values = jnp.clip(base, -1.0, 1.0)
    return values.astype(jnp.bfloat16)


def block_levels(own_key, dims, pieces, low, largest):
    level, own = 1.0, jax.random.fold_in(own_key, 6)
    for dim, parts in pieces:
        steps = jnp.exp(jax.random.uniform(jax.random.fold_in(own, dim), (parts,), jnp.float32, low / len(pieces), largest / len(pieces)))
        level = level * jnp.repeat(steps, dims[dim] // parts).reshape([-1 if axis == dim else 1 for axis in range(len(dims))])
    return level


def gaussian(stream_key, extent, spread, limit, shards=(), kind=jnp.bfloat16):
    entries = spread * jax.random.normal(stream_key, extent, jnp.float32)
    if shards:
        entries = entries * block_levels(stream_key, extent, shards, -0.22, 0.18)
    return jnp.clip(entries, -limit, limit).astype(kind)


def setup_inputs(seed: int = 0) -> dict:
    key_list = jax.random.split(jax.random.key(seed), 9)
    tokens = draw_tokens(jax.random.fold_in(key_list[8], 71), 0)
    gain = jnp.clip(1.0 + 0.15 * jax.random.normal(key_list[1], (D,), jnp.float32), 0.25, 1.75)
    qkv_weight = draw_qkv_weight(jax.random.fold_in(key_list[8], 71), 0)
    adapter_in = gaussian(key_list[3], (ADAPTERS, D, 2 * RANK), D ** -0.5, 0.125, ((0, 128), (1, 4)))
    adapter_out = gaussian(key_list[4], (ADAPTERS, 2, RANK, HEADS * HEAD), (4 * RANK) ** -0.5, 0.75, ((0, 128), (3, 4)))
    request_of = draw_request_of(jax.random.fold_in(key_list[8], 71), 0)
    adapter_of = draw_adapter_of(jax.random.fold_in(key_list[8], 71), 0)
    block_row = draw_block_row(jax.random.fold_in(key_list[8], 71), 0)
    return dict(tokens=tokens, gain=gain, qkv_weight=qkv_weight, adapter_in=adapter_in, adapter_out=adapter_out, request_of=request_of, adapter_of=adapter_of, block_row=block_row)


adapter_scale = 2.0
norm_eps = 1e-06

def root_mean_normed(rows, gain):
    wide = rows.astype(jnp.float32)
    power = lax.optimization_barrier(jnp.mean(wide * wide, axis=1, keepdims=True))
    return (wide * lax.rsqrt(power + norm_eps) * gain.astype(jnp.float32)).astype(jnp.bfloat16)

def token_slots(request_entry, adapters, offsets, capacity, total):
    count = adapters.shape[0]
    match = request_entry[:, None] == jnp.arange(count, dtype=jnp.int32)[None, :]
    adapter = lax.optimization_barrier(jnp.sum(jnp.where(match, adapters[None, :], 0), axis=1)).astype(jnp.int32)
    live = request_entry < count
    slots = jnp.where(live, adapter * capacity + offsets, total).astype(jnp.int32)
    return (slots, live)

def attend(query, keys, value, request_entry, heads, head):
    rows = query.shape[0]
    block = min(512, rows)
    margin = LMAX
    pad_k = jnp.pad(keys, ((margin, margin), (0, 0)))
    pad_v = jnp.pad(value, ((margin, margin), (0, 0)))
    pad_r = jnp.pad(request_entry, (margin, margin), constant_values=-1)
    outputs = []
    for first in range(0, rows, block):
        span = block + 2 * margin
        q_blk = query[first:first + block].reshape(block, heads, head).astype(jnp.float32)
        k_blk = pad_k[first:first + span].reshape(span, heads, head).astype(jnp.float32)
        v_blk = pad_v[first:first + span].reshape(span, heads, head).astype(jnp.float32)
        same = request_entry[first:first + block][:, None] == pad_r[first:first + span][None, :]
        scores = jnp.einsum('qhd,khd->hqk', q_blk, k_blk) * head ** (-0.5)
        scores = jnp.where(same[None], scores, -jnp.inf)
        top = lax.optimization_barrier(jnp.max(scores, axis=2, keepdims=True))
        expo = jnp.exp(scores - top)
        weights = (expo / lax.optimization_barrier(jnp.sum(expo, axis=2, keepdims=True))).astype(jnp.bfloat16)
        mixed = jnp.einsum('hqk,khd->qhd', weights.astype(jnp.float32), v_blk)
        outputs.append(mixed.reshape(block, heads * head))
    return jnp.concatenate(outputs, 0)

def reference(tokens, gain, qkv_weight, adapter_in, adapter_out, request_of, adapter_of, block_row):
    weight_all = qkv_weight.astype(jnp.float32)
    down_all = adapter_in.astype(jnp.float32)
    up_query = adapter_out[:, 0].astype(jnp.float32)
    up_value = adapter_out[:, 1].astype(jnp.float32)
    width = HEADS * HEAD

    def one_group(items):
        rows, request_entry, adapters, offsets = items
        normed = root_mean_normed(rows, gain)
        slots, live = token_slots(request_entry, adapters, offsets, CAP, SLOTS)
        buffer = jnp.zeros((SLOTS, D), jnp.bfloat16).at[slots].set(normed, mode='drop')
        buffer = buffer.reshape(ADAPTERS, CAP, D)
        part = jnp.einsum('acd,adr->acr', buffer.astype(jnp.float32), down_all)
        reduced = part.astype(jnp.bfloat16).astype(jnp.float32)
        query_slice = jnp.einsum('acr,are->ace', reduced[..., :RANK], up_query)
        value_slice = jnp.einsum('acr,are->ace', reduced[..., RANK:], up_value)
        adapter_deltas = (adapter_scale * jnp.concatenate([query_slice, value_slice], -1)).astype(jnp.bfloat16)
        adapter_deltas = adapter_deltas.reshape(SLOTS, 2 * width)
        adapter_deltas = jnp.take(adapter_deltas, slots, axis=0, mode='fill', fill_value=0)
        base = jnp.einsum('td,jde->jte', normed.astype(jnp.float32), weight_all)
        query = (base[0] + adapter_deltas[:, :width].astype(jnp.float32)).astype(jnp.bfloat16)
        keys = base[1].astype(jnp.bfloat16)
        value = (base[2] + adapter_deltas[:, width:].astype(jnp.float32)).astype(jnp.bfloat16)
        mixed = attend(query, keys, value, request_entry, HEADS, HEAD)
        return jnp.where(live[:, None], mixed, 0.0).astype(jnp.bfloat16)
    result = lax.map(one_group, (tokens.reshape(GROUPS, TOK_DEV, D), request_of, adapter_of, block_row))
    return result.reshape(TOKENS, HEADS * HEAD)
```

```python
import jax
import jax.numpy as jnp
from jax import lax
from jax.sharding import PartitionSpec as P

HEAD = 64
LMAX = 16


adapter_scale = 2.0
norm_eps = 1e-06


def root_mean_normed(rows, gain):
    wide = rows.astype(jnp.float32)
    power = jnp.mean(wide * wide, axis=1, keepdims=True)
    return (wide * lax.rsqrt(power + norm_eps) * gain).astype(jnp.bfloat16)


def attend(query, keys, value, request_entry, heads, head):
    rows = query.shape[0]
    block = min(512, rows)
    margin = LMAX
    pad_k = jnp.pad(keys, ((margin, margin), (0, 0)))
    pad_v = jnp.pad(value, ((margin, margin), (0, 0)))
    pad_r = jnp.pad(request_entry, (margin, margin), constant_values=-1)
    span = block + 2 * margin
    q_blk = query.reshape(block, heads, head)
    k_blk = pad_k.reshape(span, heads, head)
    v_blk = pad_v.reshape(span, heads, head)
    same = request_entry[:, None] == pad_r[None, :]
    scores = jnp.einsum(
        "qhd,khd->hqk", q_blk, k_blk, preferred_element_type=jnp.float32
    ) * head ** (-0.5)
    scores = jnp.where(same[None], scores, -jnp.inf)
    top = jnp.max(scores, axis=2, keepdims=True)
    expo = jnp.exp(scores - top)
    weights = (expo / jnp.sum(expo, axis=2, keepdims=True)).astype(jnp.bfloat16)
    mixed = jnp.einsum("hqk,khd->qhd", weights, v_blk, preferred_element_type=jnp.float32)
    outputs = mixed.reshape(block, heads * head)
    return outputs


def shards(tokens, gain, qkv_weight, adapter_in, adapter_out, request_of, adapter_of, block_row):
    width = tokens.shape[1]
    rank2 = adapter_in.shape[2]
    rank = rank2 // 2
    heads_width = qkv_weight.shape[2]
    packed = jnp.concatenate(
        [adapter_in.reshape(1, -1), adapter_out.reshape(1, -1)], axis=1
    )
    every = lax.all_gather(packed, "req", axis=0, tiled=True)
    n_ad = every.shape[0]
    ins = every[:, : width * rank2].reshape(n_ad, width, rank2)
    outs = every[:, width * rank2 :].reshape(n_ad, 2, rank, heads_width)

    whole = lax.all_gather(tokens, "tp", axis=1, tiled=True)
    normed = root_mean_normed(whole, gain)
    split = lax.axis_index("tp")
    own = lax.dynamic_slice_in_dim(normed, split * width, width, 1)

    request_entry = request_of[0]
    adapters = adapter_of[0]
    count = adapters.shape[0]
    rows = request_entry.shape[0]
    onehot = request_entry[:, None] == jnp.arange(count, dtype=jnp.int32)[None, :]
    live = request_entry < count

    sel_in = jnp.take(ins, adapters, axis=0)
    part = jnp.einsum("td,rdk->trk", own, sel_in, preferred_element_type=jnp.float32)
    part = jnp.sum(jnp.where(onehot[:, :, None], part, 0.0), axis=1)
    low = lax.psum(part, "tp").astype(jnp.bfloat16)

    sel_out = jnp.take(outs, adapters, axis=0)
    zero = jnp.zeros((), jnp.bfloat16)
    low_q = jnp.where(onehot[:, :, None], low[:, None, :rank], zero).reshape(rows, count * rank)
    low_v = jnp.where(onehot[:, :, None], low[:, None, rank:], zero).reshape(rows, count * rank)
    delta_q = jnp.dot(
        low_q, sel_out[:, 0].reshape(count * rank, heads_width), preferred_element_type=jnp.float32
    )
    delta_v = jnp.dot(
        low_v, sel_out[:, 1].reshape(count * rank, heads_width), preferred_element_type=jnp.float32
    )
    delta_q = (adapter_scale * delta_q).astype(jnp.bfloat16)
    delta_v = (adapter_scale * delta_v).astype(jnp.bfloat16)

    base = jnp.einsum("td,jde->jte", normed, qkv_weight, preferred_element_type=jnp.float32)
    query = (base[0] + delta_q.astype(jnp.float32)).astype(jnp.bfloat16)
    keys = base[1].astype(jnp.bfloat16)
    value = (base[2] + delta_v.astype(jnp.float32)).astype(jnp.bfloat16)
    mixed = attend(query, keys, value, request_entry, heads_width // HEAD, HEAD)
    return jnp.where(live[:, None], mixed, 0.0).astype(jnp.bfloat16)


def solution(mesh):
    in_specs = (
        P("req", "tp"),
        P(),
        P(None, None, "tp"),
        P("req", "tp", None),
        P("req", None, None, "tp"),
        P("req", None),
        P("req", None),
        P("req", None),
    )
    out_specs = P("req", "tp")
    return jax.shard_map(shards, mesh=mesh, in_specs=in_specs, out_specs=out_specs, check_vma=False)
```

```python
import jax
import jax.numpy as jnp
import numpy as np
from jax import lax
from jax.sharding import Mesh, PartitionSpec as P

HEAD = 64
LMAX = 16
LANES = 128


adapter_scale = 2.0
norm_eps = 1e-06


def attend(query, keys, value, request_entry, heads, head):
    rows = query.shape[0]
    block = min(512, rows)
    margin = LMAX
    pad_k = jnp.pad(keys, ((margin, margin), (0, 0)))
    pad_v = jnp.pad(value, ((margin, margin), (0, 0)))
    pad_r = jnp.pad(request_entry, (margin, margin), constant_values=-1)
    span = block + 2 * margin
    q_blk = query.reshape(block, heads, head)
    k_blk = pad_k.reshape(span, heads, head)
    v_blk = pad_v.reshape(span, heads, head)
    same = request_entry[:, None] == pad_r[None, :]
    scores = jnp.einsum(
        "qhd,khd->hqk", q_blk, k_blk, preferred_element_type=jnp.float32
    ) * head ** (-0.5)
    scores = jnp.where(same[None], scores, -jnp.inf)
    top = jnp.max(scores, axis=2, keepdims=True)
    expo = jnp.exp(scores - top)
    weights = (expo / jnp.sum(expo, axis=2, keepdims=True)).astype(jnp.bfloat16)
    mixed = jnp.einsum("hqk,khd->qhd", weights, v_blk, preferred_element_type=jnp.float32)
    outputs = mixed.reshape(block, heads * head)
    return outputs


def tp_shifts(value, n_tp):
    got = []
    for s in range(1, n_tp):
        perm = [(i, (i + s) % n_tp) for i in range(n_tp)]
        got.append(lax.ppermute(value, "tp", perm))
    return got


def shards(tokens, gain, qkv_weight, adapter_in, adapter_out, request_of, adapter_of, block_row):
    width = tokens.shape[1]
    rank2 = adapter_in.shape[2]
    rank = rank2 // 2
    heads_width = qkv_weight.shape[2]
    n_tp = lax.axis_size("tp")
    n_y, n_z, n_c = lax.axis_size("ry"), lax.axis_size("rz"), lax.axis_size("rc")
    split = lax.axis_index("tp")

    in_rows = adapter_in.size // LANES
    packed = jnp.concatenate(
        [adapter_in.reshape(in_rows, LANES), adapter_out.reshape(-1, LANES)], axis=0
    )
    per = packed.shape[0]
    every = lax.all_gather(packed, "rz", axis=0, tiled=True)
    every = lax.all_gather(every, "ry", axis=0, tiled=True)
    every = lax.all_gather(every, "rc", axis=0, tiled=True)
    every = every.reshape(n_c * n_y * n_z, per, LANES)

    request_entry = request_of[0]
    adapters = adapter_of[0]
    count = adapters.shape[0]
    rows = request_entry.shape[0]
    onehot = request_entry[:, None] == jnp.arange(count, dtype=jnp.int32)[None, :]
    live = request_entry < count

    a_c = adapters % n_c
    a_z = (adapters // n_c) % n_z
    a_y = adapters // (n_c * n_z)
    place = (a_c * n_y + a_y) * n_z + a_z
    sel = jnp.take(every, place, axis=0)
    sel_in = sel[:, :in_rows].reshape(count, width, rank2)
    sel_out = sel[:, in_rows:].reshape(count, 2, rank, heads_width)

    pieces = [tokens] + tp_shifts(tokens, n_tp)
    wide = [p.astype(jnp.float32) for p in pieces]
    power = sum(jnp.sum(w * w, axis=1, keepdims=True) for w in wide) / (width * n_tp)
    scale = lax.rsqrt(power + norm_eps)
    normed = jnp.zeros((rows, width * n_tp), jnp.bfloat16)
    own = None
    for s, w in enumerate(wide):
        src = (split - s) % n_tp
        g = lax.dynamic_slice_in_dim(gain, src * width, width)
        piece = (w * scale * g).astype(jnp.bfloat16)
        if s == 0:
            own = piece
        normed = lax.dynamic_update_slice_in_dim(normed, piece, src * width, 1)

    part = jnp.einsum("td,rdk->trk", own, sel_in, preferred_element_type=jnp.float32)
    part = jnp.sum(jnp.where(onehot[:, :, None], part, 0.0), axis=1)
    total = part
    for p in tp_shifts(part, n_tp):
        total = total + p
    low = total.astype(jnp.bfloat16)

    zero = jnp.zeros((), jnp.bfloat16)
    low_q = jnp.where(onehot[:, :, None], low[:, None, :rank], zero).reshape(rows, count * rank)
    low_v = jnp.where(onehot[:, :, None], low[:, None, rank:], zero).reshape(rows, count * rank)
    delta_q = jnp.dot(
        low_q, sel_out[:, 0].reshape(count * rank, heads_width), preferred_element_type=jnp.float32
    )
    delta_v = jnp.dot(
        low_v, sel_out[:, 1].reshape(count * rank, heads_width), preferred_element_type=jnp.float32
    )
    delta_q = (adapter_scale * delta_q).astype(jnp.bfloat16)
    delta_v = (adapter_scale * delta_v).astype(jnp.bfloat16)

    base = jnp.einsum("td,jde->jte", normed, qkv_weight, preferred_element_type=jnp.float32)
    query = (base[0] + delta_q.astype(jnp.float32)).astype(jnp.bfloat16)
    keys = base[1].astype(jnp.bfloat16)
    value = (base[2] + delta_v.astype(jnp.float32)).astype(jnp.bfloat16)
    mixed = attend(query, keys, value, request_entry, heads_width // HEAD, HEAD)
    return jnp.where(live[:, None], mixed, 0.0).astype(jnp.bfloat16)


def torus_mesh(mesh):
    devs = mesh.devices
    n_req, n_tp = devs.shape
    col = devs[:, 0]
    try:
        n_y = len({d.coords[1] for d in col})
        n_z = len({d.coords[2] for d in col})
        n_c = len({d.core_on_chip for d in col})
    except AttributeError:
        n_y, n_z, n_c = n_req, 1, 1
    if n_y * n_z * n_c != n_req:
        n_y, n_z, n_c = n_req, 1, 1
    return Mesh(np.asarray(devs).reshape(n_y, n_z, n_c, n_tp), ("ry", "rz", "rc", "tp"))


def solution(mesh):
    grid = torus_mesh(mesh)
    req = ("ry", "rz", "rc")
    in_specs = (
        P(req, "tp"),
        P(),
        P(None, None, "tp"),
        P(req, "tp", None),
        P(req, None, None, "tp"),
        P(req, None),
        P(req, None),
        P(req, None),
    )
    out_specs = P(req, "tp")
    return jax.shard_map(shards, mesh=grid, in_specs=in_specs, out_specs=out_specs, check_vma=False)
```

```python
import jax
import jax.numpy as jnp
import numpy as np
from jax import lax
from jax.sharding import Mesh, PartitionSpec as P

HEAD = 64
LMAX = 16
LANES = 128


adapter_scale = 2.0
norm_eps = 1e-06


def attend(query, keys, value, request_entry, heads, head):
    rows = query.shape[0]
    block = min(512, rows)
    margin = LMAX
    pad_k = jnp.pad(keys, ((margin, margin), (0, 0)))
    pad_v = jnp.pad(value, ((margin, margin), (0, 0)))
    pad_r = jnp.pad(request_entry, (margin, margin), constant_values=-1)
    span = block + 2 * margin
    q_blk = query.reshape(block, heads, head)
    k_blk = pad_k.reshape(span, heads, head)
    v_blk = pad_v.reshape(span, heads, head)
    same = request_entry[:, None] == pad_r[None, :]
    scores = jnp.einsum(
        "qhd,khd->hqk", q_blk, k_blk, preferred_element_type=jnp.float32
    ) * head ** (-0.5)
    scores = jnp.where(same[None], scores, -jnp.inf)
    top = jnp.max(scores, axis=2, keepdims=True)
    expo = jnp.exp(scores - top)
    weights = (expo / jnp.sum(expo, axis=2, keepdims=True)).astype(jnp.bfloat16)
    mixed = jnp.einsum("hqk,khd->qhd", weights, v_blk, preferred_element_type=jnp.float32)
    outputs = mixed.reshape(block, heads * head)
    return outputs


def tp_shifts(value, n_tp):
    got = []
    for s in range(1, n_tp):
        perm = [(i, (i + s) % n_tp) for i in range(n_tp)]
        got.append(lax.ppermute(value, "tp", perm))
    return got


def shards(tokens, gain, qkv_weight, adapter_in, adapter_out, request_of, adapter_of, block_row):
    width = tokens.shape[1]
    rank2 = adapter_in.shape[2]
    rank = rank2 // 2
    heads_width = qkv_weight.shape[2]
    n_tp = lax.axis_size("tp")
    n_y, n_z, n_c = lax.axis_size("ry"), lax.axis_size("rz"), lax.axis_size("rc")
    split = lax.axis_index("tp")

    in_rows = adapter_in.size // LANES
    packed = jnp.concatenate(
        [adapter_in.reshape(in_rows, LANES), adapter_out.reshape(-1, LANES)], axis=0
    )
    per = packed.shape[0]
    every = lax.all_gather(packed, ("ry", "rz"), axis=0, tiled=True)
    every = lax.all_gather(every, "rc", axis=0, tiled=True)
    every = every.reshape(n_c * n_y * n_z, per, LANES)

    request_entry = request_of[0]
    adapters = adapter_of[0]
    count = adapters.shape[0]
    rows = request_entry.shape[0]
    onehot = request_entry[:, None] == jnp.arange(count, dtype=jnp.int32)[None, :]
    live = request_entry < count

    a_c = adapters % n_c
    a_z = (adapters // n_c) % n_z
    a_y = adapters // (n_c * n_z)
    place = (a_c * n_y + a_y) * n_z + a_z
    sel = jnp.take(every, place, axis=0)
    sel_in = sel[:, :in_rows].reshape(count, width, rank2)
    sel_out = sel[:, in_rows:].reshape(count, 2, rank, heads_width)

    pieces = [tokens] + tp_shifts(tokens, n_tp)
    wide = [p.astype(jnp.float32) for p in pieces]
    power = sum(jnp.sum(w * w, axis=1, keepdims=True) for w in wide) / (width * n_tp)
    scale = lax.rsqrt(power + norm_eps)
    normed = jnp.zeros((rows, width * n_tp), jnp.bfloat16)
    own = None
    for s, w in enumerate(wide):
        src = (split - s) % n_tp
        g = lax.dynamic_slice_in_dim(gain, src * width, width)
        piece = (w * scale * g).astype(jnp.bfloat16)
        if s == 0:
            own = piece
        normed = lax.dynamic_update_slice_in_dim(normed, piece, src * width, 1)

    part = jnp.einsum("td,rdk->trk", own, sel_in, preferred_element_type=jnp.float32)
    part = jnp.sum(jnp.where(onehot[:, :, None], part, 0.0), axis=1)
    total = part
    for p in tp_shifts(part, n_tp):
        total = total + p
    low = total.astype(jnp.bfloat16)

    zero = jnp.zeros((), jnp.bfloat16)
    low_q = jnp.where(onehot[:, :, None], low[:, None, :rank], zero).reshape(rows, count * rank)
    low_v = jnp.where(onehot[:, :, None], low[:, None, rank:], zero).reshape(rows, count * rank)
    delta_q = jnp.dot(
        low_q, sel_out[:, 0].reshape(count * rank, heads_width), preferred_element_type=jnp.float32
    )
    delta_v = jnp.dot(
        low_v, sel_out[:, 1].reshape(count * rank, heads_width), preferred_element_type=jnp.float32
    )
    delta_q = lax.reduce_precision(adapter_scale * delta_q, exponent_bits=8, mantissa_bits=7)
    delta_v = lax.reduce_precision(adapter_scale * delta_v, exponent_bits=8, mantissa_bits=7)

    base = jnp.einsum("td,jde->jte", normed, qkv_weight, preferred_element_type=jnp.float32)
    query = (base[0] + delta_q).astype(jnp.bfloat16)
    keys = base[1].astype(jnp.bfloat16)
    value = (base[2] + delta_v).astype(jnp.bfloat16)
    mixed = attend(query, keys, value, request_entry, heads_width // HEAD, HEAD)
    return jnp.where(live[:, None], mixed, 0.0).astype(jnp.bfloat16)


def torus_mesh(mesh):
    devs = mesh.devices
    n_req, n_tp = devs.shape
    col = devs[:, 0]
    try:
        n_y = len({d.coords[1] for d in col})
        n_z = len({d.coords[2] for d in col})
        n_c = len({d.core_on_chip for d in col})
    except AttributeError:
        n_y, n_z, n_c = n_req, 1, 1
    if n_y * n_z * n_c != n_req:
        n_y, n_z, n_c = n_req, 1, 1
    return Mesh(np.asarray(devs).reshape(n_y, n_z, n_c, n_tp), ("ry", "rz", "rc", "tp"))


def solution(mesh):
    grid = torus_mesh(mesh)
    req = ("ry", "rz", "rc")
    in_specs = (
        P(req, "tp"),
        P(),
        P(None, None, "tp"),
        P(req, "tp", None),
        P(req, None, None, "tp"),
        P(req, None),
        P(req, None),
        P(req, None),
    )
    out_specs = P(req, "tp")
    return jax.shard_map(shards, mesh=grid, in_specs=in_specs, out_specs=out_specs, check_vma=False)
```

```python
import jax
import jax.numpy as jnp
import numpy as np
from jax import lax
from jax.sharding import Mesh, PartitionSpec as P

HEAD = 64
LMAX = 16
LANES = 128


adapter_scale = 2.0
norm_eps = 1e-06


def attend(query, keys, value, request_entry, heads, head):
    rows = query.shape[0]
    block = min(512, rows)
    margin = LMAX
    pad_k = jnp.pad(keys, ((margin, margin), (0, 0)))
    pad_v = jnp.pad(value, ((margin, margin), (0, 0)))
    pad_r = jnp.pad(request_entry, (margin, margin), constant_values=-1)
    span = block + 2 * margin
    q_blk = query.reshape(block, heads, head)
    k_blk = pad_k.reshape(span, heads, head)
    v_blk = pad_v.reshape(span, heads, head)
    same = request_entry[:, None] == pad_r[None, :]
    scores = jnp.einsum(
        "qhd,khd->hqk", q_blk, k_blk, preferred_element_type=jnp.float32
    ) * head ** (-0.5)
    scores = jnp.where(same[None], scores, -jnp.inf)
    top = jnp.max(scores, axis=2, keepdims=True)
    expo = jnp.exp(scores - top)
    weights = (expo / jnp.sum(expo, axis=2, keepdims=True)).astype(jnp.bfloat16)
    mixed = jnp.einsum("hqk,khd->qhd", weights, v_blk, preferred_element_type=jnp.float32)
    outputs = mixed.reshape(block, heads * head)
    return outputs


def exchange(value, axis, pairs):
    return lax.ppermute(value, axis, pairs)


def ring_gather(value, axis, n):
    rel = [None] * n
    rel[0] = value
    cw = value
    ccw = value
    for s in range(1, n // 2 + 1):
        cw = exchange(cw, axis, [(i, (i + 1) % n) for i in range(n)])
        rel[(n - s) % n] = cw
        if s < n - s:
            ccw = exchange(ccw, axis, [(i, (i - 1) % n) for i in range(n)])
            rel[s] = ccw
    return jnp.stack(rel)


def doubling_sources(n):
    return n > 1 and (n & (n - 1)) == 0


def shards(tokens, gain, qkv_weight, adapter_in, adapter_out, request_of, adapter_of, block_row):
    width = tokens.shape[1]
    rank2 = adapter_in.shape[2]
    rank = rank2 // 2
    heads_width = qkv_weight.shape[2]
    n_tp = lax.axis_size("tp")
    n_y, n_z, n_c = lax.axis_size("ry"), lax.axis_size("rz"), lax.axis_size("rc")
    split = lax.axis_index("tp")
    my_y, my_z, my_c = lax.axis_index("ry"), lax.axis_index("rz"), lax.axis_index("rc")

    request_entry = request_of[0]
    adapters = adapter_of[0]
    count = adapters.shape[0]
    rows = request_entry.shape[0]
    onehot = request_entry[:, None] == jnp.arange(count, dtype=jnp.int32)[None, :]
    live = request_entry < count

    if doubling_sources(n_tp):
        pieces, sources = [tokens], [split]
        k = 1
        while k < n_tp:
            got = exchange(jnp.stack(pieces), "tp", [(i, i ^ k) for i in range(n_tp)])
            pieces = pieces + [got[j] for j in range(got.shape[0])]
            sources = sources + [src ^ k for src in sources]
            k *= 2
    else:
        pieces, sources = [tokens], [split]
        for s in range(1, n_tp):
            pieces.append(exchange(tokens, "tp", [(i, (i + s) % n_tp) for i in range(n_tp)]))
            sources.append((split - s) % n_tp)

    in_rows = adapter_in.size // LANES
    packed = jnp.concatenate(
        [adapter_in.reshape(in_rows, LANES), adapter_out.reshape(-1, LANES)], axis=0
    )
    per = packed.shape[0]
    if n_c > 1:
        partner = exchange(adapters, "rc", [(i, (i + 1) % n_c) for i in range(n_c)])
    every = ring_gather(packed, "rz", n_z)
    every = ring_gather(every, "ry", n_y).reshape(n_y * n_z, per, LANES)

    def place(ads):
        a_c = ads % n_c
        a_z = (ads // n_c) % n_z
        a_y = ads // (n_c * n_z)
        return ((a_y - my_y) % n_y) * n_z + (a_z - my_z) % n_z, a_c

    here, a_c = place(adapters)
    sel = jnp.take(every, here, axis=0)
    if n_c > 1:
        there, _ = place(partner)
        sent = exchange(jnp.take(every, there, axis=0), "rc", [(i, (i - 1) % n_c) for i in range(n_c)])
        sel = jnp.where((a_c == my_c)[:, None, None], sel, sent)
    sel_in = sel[:, :in_rows].reshape(count, width, rank2)
    sel_out = sel[:, in_rows:].reshape(count, 2, rank, heads_width)

    wide = [p.astype(jnp.float32) for p in pieces]
    power = sum(jnp.sum(w * w, axis=1, keepdims=True) for w in wide) / (width * n_tp)
    scale = lax.rsqrt(power + norm_eps)
    normed = jnp.zeros((rows, width * n_tp), jnp.bfloat16)
    own = None
    for s, (w, src) in enumerate(zip(wide, sources)):
        g = lax.dynamic_slice_in_dim(gain, src * width, width)
        piece = (w * scale * g).astype(jnp.bfloat16)
        if s == 0:
            own = piece
        normed = lax.dynamic_update_slice_in_dim(normed, piece, src * width, 1)

    part = jnp.einsum("td,rdk->trk", own, sel_in, preferred_element_type=jnp.float32)
    part = jnp.sum(jnp.where(onehot[:, :, None], part, 0.0), axis=1)
    if doubling_sources(n_tp):
        total = part
        k = 1
        while k < n_tp:
            total = total + exchange(total, "tp", [(i, i ^ k) for i in range(n_tp)])
            k *= 2
    else:
        total = part
        for s in range(1, n_tp):
            total = total + exchange(part, "tp", [(i, (i + s) % n_tp) for i in range(n_tp)])
    low = total.astype(jnp.bfloat16)

    zero = jnp.zeros((), jnp.bfloat16)
    low_q = jnp.where(onehot[:, :, None], low[:, None, :rank], zero).reshape(rows, count * rank)
    low_v = jnp.where(onehot[:, :, None], low[:, None, rank:], zero).reshape(rows, count * rank)
    delta_q = jnp.dot(
        low_q, sel_out[:, 0].reshape(count * rank, heads_width), preferred_element_type=jnp.float32
    )
    delta_v = jnp.dot(
        low_v, sel_out[:, 1].reshape(count * rank, heads_width), preferred_element_type=jnp.float32
    )
    delta_q = lax.reduce_precision(adapter_scale * delta_q, exponent_bits=8, mantissa_bits=7)
    delta_v = lax.reduce_precision(adapter_scale * delta_v, exponent_bits=8, mantissa_bits=7)

    base = jnp.einsum("td,jde->jte", normed, qkv_weight, preferred_element_type=jnp.float32)
    query = (base[0] + delta_q).astype(jnp.bfloat16)
    keys = base[1].astype(jnp.bfloat16)
    value = (base[2] + delta_v).astype(jnp.bfloat16)
    mixed = attend(query, keys, value, request_entry, heads_width // HEAD, HEAD)
    return jnp.where(live[:, None], mixed, 0.0).astype(jnp.bfloat16)


def torus_mesh(mesh):
    devs = mesh.devices
    n_req, n_tp = devs.shape
    col = devs[:, 0]
    try:
        n_y = len({d.coords[1] for d in col})
        n_z = len({d.coords[2] for d in col})
        n_c = len({d.core_on_chip for d in col})
    except AttributeError:
        n_y, n_z, n_c = n_req, 1, 1
    if n_y * n_z * n_c != n_req:
        n_y, n_z, n_c = n_req, 1, 1
    return Mesh(np.asarray(devs).reshape(n_y, n_z, n_c, n_tp), ("ry", "rz", "rc", "tp"))


def solution(mesh):
    grid = torus_mesh(mesh)
    req = ("ry", "rz", "rc")
    in_specs = (
        P(req, "tp"),
        P(),
        P(None, None, "tp"),
        P(req, "tp", None),
        P(req, None, None, "tp"),
        P(req, None),
        P(req, None),
        P(req, None),
    )
    out_specs = P(req, "tp")
    return jax.shard_map(shards, mesh=grid, in_specs=in_specs, out_specs=out_specs, check_vma=False)
```

```python
import jax
import jax.numpy as jnp
import numpy as np
from jax import lax
from jax.sharding import Mesh, PartitionSpec as P

HEAD = 64
LMAX = 16
LANES = 128


adapter_scale = 2.0
norm_eps = 1e-06


def attend(query, keys, value, request_entry, heads, head):
    rows = query.shape[0]
    block = min(512, rows)
    margin = LMAX
    pad_k = jnp.pad(keys, ((margin, margin), (0, 0)))
    pad_v = jnp.pad(value, ((margin, margin), (0, 0)))
    pad_r = jnp.pad(request_entry, (margin, margin), constant_values=-1)
    span = block + 2 * margin
    q_blk = query.reshape(block, heads, head)
    k_blk = pad_k.reshape(span, heads, head)
    v_blk = pad_v.reshape(span, heads, head)
    same = request_entry[:, None] == pad_r[None, :]
    scores = jnp.einsum(
        "qhd,khd->hqk", q_blk, k_blk, preferred_element_type=jnp.float32
    ) * head ** (-0.5)
    scores = jnp.where(same[None], scores, -jnp.inf)
    top = jnp.max(scores, axis=2, keepdims=True)
    expo = jnp.exp(scores - top)
    weights = (expo / jnp.sum(expo, axis=2, keepdims=True)).astype(jnp.bfloat16)
    mixed = jnp.einsum("hqk,khd->qhd", weights, v_blk, preferred_element_type=jnp.float32)
    outputs = mixed.reshape(block, heads * head)
    return outputs


def exchange(value, axis, pairs):
    return lax.ppermute(value, axis, pairs)


def ring_gather(value, axis, n):
    rel = [None] * n
    rel[0] = value
    cw = value
    ccw = value
    for s in range(1, n // 2 + 1):
        cw = exchange(cw, axis, [(i, (i + 1) % n) for i in range(n)])
        rel[(n - s) % n] = cw
        if s < n - s:
            ccw = exchange(ccw, axis, [(i, (i - 1) % n) for i in range(n)])
            rel[s] = ccw
    return jnp.stack(rel)


def doubling_sources(n):
    return n > 1 and (n & (n - 1)) == 0


def shards(tokens, gain, qkv_weight, adapter_in, adapter_out, request_of, adapter_of, block_row):
    width = tokens.shape[1]
    rank2 = adapter_in.shape[2]
    rank = rank2 // 2
    heads_width = qkv_weight.shape[2]
    n_tp = lax.axis_size("tp")
    n_y, n_z, n_c = lax.axis_size("ry"), lax.axis_size("rz"), lax.axis_size("rc")
    split = lax.axis_index("tp")
    my_y, my_z, my_c = lax.axis_index("ry"), lax.axis_index("rz"), lax.axis_index("rc")

    request_entry = request_of[0]
    adapters = adapter_of[0]
    count = adapters.shape[0]
    rows = request_entry.shape[0]
    onehot = request_entry[:, None] == jnp.arange(count, dtype=jnp.int32)[None, :]
    live = request_entry < count

    if doubling_sources(n_tp):
        pieces, sources = [tokens], [split]
        k = 1
        while k < n_tp:
            got = exchange(jnp.stack(pieces), "tp", [(i, i ^ k) for i in range(n_tp)])
            pieces = pieces + [got[j] for j in range(got.shape[0])]
            sources = sources + [src ^ k for src in sources]
            k *= 2
    else:
        pieces, sources = [tokens], [split]
        for s in range(1, n_tp):
            pieces.append(exchange(tokens, "tp", [(i, (i + s) % n_tp) for i in range(n_tp)]))
            sources.append((split - s) % n_tp)

    in_rows = adapter_in.size // LANES
    packed = jnp.concatenate(
        [adapter_in.reshape(in_rows, LANES), adapter_out.reshape(-1, LANES)], axis=0
    )
    per = packed.shape[0]
    if n_c > 1:
        partner = exchange(adapters, "rc", [(i, (i + 1) % n_c) for i in range(n_c)])
    every = lax.all_gather(packed, "rz", axis=0, tiled=True)
    every = lax.all_gather(every, "ry", axis=0, tiled=True).reshape(n_y * n_z, per, LANES)

    def place(ads):
        a_c = ads % n_c
        a_z = (ads // n_c) % n_z
        a_y = ads // (n_c * n_z)
        return a_y * n_z + a_z, a_c

    here, a_c = place(adapters)
    sel = jnp.take(every, here, axis=0)
    if n_c > 1:
        there, _ = place(partner)
        sent = exchange(jnp.take(every, there, axis=0), "rc", [(i, (i - 1) % n_c) for i in range(n_c)])
        sel = jnp.where((a_c == my_c)[:, None, None], sel, sent)
    sel_in = sel[:, :in_rows].reshape(count, width, rank2)
    sel_out = sel[:, in_rows:].reshape(count, 2, rank, heads_width)

    wide = [p.astype(jnp.float32) for p in pieces]
    power = sum(jnp.sum(w * w, axis=1, keepdims=True) for w in wide) / (width * n_tp)
    scale = lax.rsqrt(power + norm_eps)
    normed = jnp.zeros((rows, width * n_tp), jnp.bfloat16)
    own = None
    for s, (w, src) in enumerate(zip(wide, sources)):
        g = lax.dynamic_slice_in_dim(gain, src * width, width)
        piece = (w * scale * g).astype(jnp.bfloat16)
        if s == 0:
            own = piece
        normed = lax.dynamic_update_slice_in_dim(normed, piece, src * width, 1)

    part = jnp.einsum("td,rdk->trk", own, sel_in, preferred_element_type=jnp.float32)
    part = jnp.sum(jnp.where(onehot[:, :, None], part, 0.0), axis=1)
    if doubling_sources(n_tp):
        total = part
        k = 1
        while k < n_tp:
            total = total + exchange(total, "tp", [(i, i ^ k) for i in range(n_tp)])
            k *= 2
    else:
        total = part
        for s in range(1, n_tp):
            total = total + exchange(part, "tp", [(i, (i + s) % n_tp) for i in range(n_tp)])
    low = total.astype(jnp.bfloat16)

    zero = jnp.zeros((), jnp.bfloat16)
    low_q = jnp.where(onehot[:, :, None], low[:, None, :rank], zero).reshape(rows, count * rank)
    low_v = jnp.where(onehot[:, :, None], low[:, None, rank:], zero).reshape(rows, count * rank)
    delta_q = jnp.dot(
        low_q, sel_out[:, 0].reshape(count * rank, heads_width), preferred_element_type=jnp.float32
    )
    delta_v = jnp.dot(
        low_v, sel_out[:, 1].reshape(count * rank, heads_width), preferred_element_type=jnp.float32
    )
    delta_q = lax.reduce_precision(adapter_scale * delta_q, exponent_bits=8, mantissa_bits=7)
    delta_v = lax.reduce_precision(adapter_scale * delta_v, exponent_bits=8, mantissa_bits=7)

    base = jnp.einsum("td,jde->jte", normed, qkv_weight, preferred_element_type=jnp.float32)
    query = (base[0] + delta_q).astype(jnp.bfloat16)
    keys = base[1].astype(jnp.bfloat16)
    value = (base[2] + delta_v).astype(jnp.bfloat16)
    mixed = attend(query, keys, value, request_entry, heads_width // HEAD, HEAD)
    return jnp.where(live[:, None], mixed, 0.0).astype(jnp.bfloat16)


def torus_mesh(mesh):
    devs = mesh.devices
    n_req, n_tp = devs.shape
    col = devs[:, 0]
    try:
        n_y = len({d.coords[1] for d in col})
        n_z = len({d.coords[2] for d in col})
        n_c = len({d.core_on_chip for d in col})
    except AttributeError:
        n_y, n_z, n_c = n_req, 1, 1
    if n_y * n_z * n_c != n_req:
        n_y, n_z, n_c = n_req, 1, 1
    return Mesh(np.asarray(devs).reshape(n_y, n_z, n_c, n_tp), ("ry", "rz", "rc", "tp"))


def solution(mesh):
    grid = torus_mesh(mesh)
    req = ("ry", "rz", "rc")
    in_specs = (
        P(req, "tp"),
        P(),
        P(None, None, "tp"),
        P(req, "tp", None),
        P(req, None, None, "tp"),
        P(req, None),
        P(req, None),
        P(req, None),
    )
    out_specs = P(req, "tp")
    return jax.shard_map(shards, mesh=grid, in_specs=in_specs, out_specs=out_specs, check_vma=False)
```

```python
import jax
import jax.numpy as jnp
import numpy as np
from jax import lax
from jax.sharding import Mesh, PartitionSpec as P

HEAD = 64
LMAX = 16
LANES = 128


adapter_scale = 2.0
norm_eps = 1e-06


def attend(query, keys, value, request_entry, heads, head):
    rows = query.shape[0]
    block = min(512, rows)
    margin = LMAX
    pad_k = jnp.pad(keys, ((margin, margin), (0, 0)))
    pad_v = jnp.pad(value, ((margin, margin), (0, 0)))
    pad_r = jnp.pad(request_entry, (margin, margin), constant_values=-1)
    span = block + 2 * margin
    q_blk = query.reshape(block, heads, head)
    k_blk = pad_k.reshape(span, heads, head)
    v_blk = pad_v.reshape(span, heads, head)
    same = request_entry[:, None] == pad_r[None, :]
    scores = jnp.einsum(
        "qhd,khd->hqk", q_blk, k_blk, preferred_element_type=jnp.float32
    ) * head ** (-0.5)
    scores = jnp.where(same[None], scores, -jnp.inf)
    top = jnp.max(scores, axis=2, keepdims=True)
    expo = jnp.exp(scores - top)
    weights = (expo / jnp.sum(expo, axis=2, keepdims=True)).astype(jnp.bfloat16)
    mixed = jnp.einsum("hqk,khd->qhd", weights, v_blk, preferred_element_type=jnp.float32)
    outputs = mixed.reshape(block, heads * head)
    return outputs


def exchange(value, axis, pairs):
    return lax.ppermute(value, axis, pairs)


def ring_gather(value, axis, n):
    rel = [None] * n
    rel[0] = value
    cw = value
    ccw = value
    for s in range(1, n // 2 + 1):
        cw = exchange(cw, axis, [(i, (i + 1) % n) for i in range(n)])
        rel[(n - s) % n] = cw
        if s < n - s:
            ccw = exchange(ccw, axis, [(i, (i - 1) % n) for i in range(n)])
            rel[s] = ccw
    return jnp.stack(rel)


def doubling_sources(n):
    return n > 1 and (n & (n - 1)) == 0


def shards(tokens, gain, qkv_weight, adapter_in, adapter_out, request_of, adapter_of, block_row):
    width = tokens.shape[1]
    rank2 = adapter_in.shape[2]
    rank = rank2 // 2
    heads_width = qkv_weight.shape[2]
    n_tp = lax.axis_size("tp")
    n_y, n_z, n_c = lax.axis_size("ry"), lax.axis_size("rz"), lax.axis_size("rc")
    split = lax.axis_index("tp")
    my_y, my_z, my_c = lax.axis_index("ry"), lax.axis_index("rz"), lax.axis_index("rc")

    request_entry = request_of[0]
    adapters = adapter_of[0]
    count = adapters.shape[0]
    rows = request_entry.shape[0]
    onehot = request_entry[:, None] == jnp.arange(count, dtype=jnp.int32)[None, :]
    live = request_entry < count

    if doubling_sources(n_tp):
        pieces, sources = [tokens], [split]
        k = 1
        while k < n_tp:
            got = exchange(jnp.stack(pieces), "tp", [(i, i ^ k) for i in range(n_tp)])
            pieces = pieces + [got[j] for j in range(got.shape[0])]
            sources = sources + [src ^ k for src in sources]
            k *= 2
    else:
        pieces, sources = [tokens], [split]
        for s in range(1, n_tp):
            pieces.append(exchange(tokens, "tp", [(i, (i + s) % n_tp) for i in range(n_tp)]))
            sources.append((split - s) % n_tp)

    n_in = adapter_in.shape[1]
    lane_w = 2 * heads_width
    down_t = adapter_in[0].T
    up_rows = adapter_out[0].reshape(2 * rank // 2, lane_w)
    packed = jnp.concatenate([down_t, up_rows], axis=0)
    per = packed.shape[0]
    if n_c > 1:
        partner = exchange(adapters, "rc", [(i, (i + 1) % n_c) for i in range(n_c)])
    every = lax.all_to_all(
        jnp.broadcast_to(packed[None], (n_z,) + packed.shape).reshape(n_z * per, lane_w),
        "rz", split_axis=0, concat_axis=0, tiled=True,
    )
    every = lax.all_gather(every, "ry", axis=0, tiled=True).reshape(n_y * n_z, per, lane_w)

    def place(ads):
        a_c = ads % n_c
        a_z = (ads // n_c) % n_z
        a_y = ads // (n_c * n_z)
        return a_y * n_z + a_z, a_c

    here, a_c = place(adapters)
    if n_c > 1:
        there, _ = place(partner)
        for_partner = jnp.take(every, there, axis=0)
        every, for_partner = lax.optimization_barrier((every, for_partner))
        sent = exchange(for_partner, "rc", [(i, (i - 1) % n_c) for i in range(n_c)])
        sel = jnp.take(every, here, axis=0)
        sel = jnp.where((a_c == my_c)[:, None, None], sel, sent)
    else:
        sel = jnp.take(every, here, axis=0)
    sel_in = sel[:, :rank2]
    sel_out = sel[:, rank2:].reshape(count, 2, rank // 2, lane_w)

    wide = [p.astype(jnp.float32) for p in pieces]
    power = sum(jnp.sum(w * w, axis=1, keepdims=True) for w in wide) / (width * n_tp)
    scale = lax.rsqrt(power + norm_eps)
    normed = jnp.zeros((rows, width * n_tp), jnp.bfloat16)
    own = None
    for s, (w, src) in enumerate(zip(wide, sources)):
        g = lax.dynamic_slice_in_dim(gain, src * width, width)
        piece = (w * scale * g).astype(jnp.bfloat16)
        if s == 0:
            own = piece
        normed = lax.dynamic_update_slice_in_dim(normed, piece, src * width, 1)

    part = jnp.einsum("td,rkd->trk", own, sel_in, preferred_element_type=jnp.float32)
    part = jnp.sum(jnp.where(onehot[:, :, None], part, 0.0), axis=1)
    if doubling_sources(n_tp):
        total = part
        k = 1
        while k < n_tp:
            total = total + exchange(total, "tp", [(i, i ^ k) for i in range(n_tp)])
            k *= 2
    else:
        total = part
        for s in range(1, n_tp):
            total = total + exchange(part, "tp", [(i, (i + s) % n_tp) for i in range(n_tp)])
    low = total.astype(jnp.bfloat16)

    zero = jnp.zeros((), jnp.bfloat16)
    low_q = jnp.where(onehot[:, :, None], low[:, None, :rank], zero).reshape(rows, count * rank)
    low_v = jnp.where(onehot[:, :, None], low[:, None, rank:], zero).reshape(rows, count * rank)
    def up(low_m, m):
        got = None
        for h in range(2):
            lhs = low_m.reshape(rows, count, rank // 2, 2)[..., h].reshape(rows, count * rank // 2)
            rhs = sel_out[:, m, :, h * heads_width:(h + 1) * heads_width].reshape(count * rank // 2, heads_width)
            term = jnp.dot(lhs, rhs, preferred_element_type=jnp.float32)
            got = term if got is None else got + term
        return got

    delta_q = up(low_q, 0)
    delta_v = up(low_v, 1)
    delta_q = lax.reduce_precision(adapter_scale * delta_q, exponent_bits=8, mantissa_bits=7)
    delta_v = lax.reduce_precision(adapter_scale * delta_v, exponent_bits=8, mantissa_bits=7)

    base = jnp.einsum("td,jde->jte", normed, qkv_weight, preferred_element_type=jnp.float32)
    query = (base[0] + delta_q).astype(jnp.bfloat16)
    keys = base[1].astype(jnp.bfloat16)
    value = (base[2] + delta_v).astype(jnp.bfloat16)
    mixed = attend(query, keys, value, request_entry, heads_width // HEAD, HEAD)
    return jnp.where(live[:, None], mixed, 0.0).astype(jnp.bfloat16)


def torus_mesh(mesh):
    devs = mesh.devices
    n_req, n_tp = devs.shape
    col = devs[:, 0]
    try:
        n_y = len({d.coords[1] for d in col})
        n_z = len({d.coords[2] for d in col})
        n_c = len({d.core_on_chip for d in col})
    except AttributeError:
        n_y, n_z, n_c = n_req, 1, 1
    if n_y * n_z * n_c != n_req:
        n_y, n_z, n_c = n_req, 1, 1
    return Mesh(np.asarray(devs).reshape(n_y, n_z, n_c, n_tp), ("ry", "rz", "rc", "tp"))


def solution(mesh):
    grid = torus_mesh(mesh)
    req = ("ry", "rz", "rc")
    in_specs = (
        P(req, "tp"),
        P(),
        P(None, None, "tp"),
        P(req, "tp", None),
        P(req, None, None, "tp"),
        P(req, None),
        P(req, None),
        P(req, None),
    )
    out_specs = P(req, "tp")
    return jax.shard_map(shards, mesh=grid, in_specs=in_specs, out_specs=out_specs, check_vma=False)
```

```python
import jax
import jax.numpy as jnp
import numpy as np
from jax import lax
from jax.sharding import Mesh, PartitionSpec as P

HEAD = 64
LMAX = 16
LANES = 128


adapter_scale = 2.0
norm_eps = 1e-06


def attend(query, keys, value, request_entry, heads, head):
    rows = query.shape[0]
    block = min(512, rows)
    margin = LMAX
    pad_k = jnp.pad(keys, ((margin, margin), (0, 0)))
    pad_v = jnp.pad(value, ((margin, margin), (0, 0)))
    pad_r = jnp.pad(request_entry, (margin, margin), constant_values=-1)
    span = block + 2 * margin
    q_blk = query.reshape(block, heads, head)
    k_blk = pad_k.reshape(span, heads, head)
    v_blk = pad_v.reshape(span, heads, head)
    same = request_entry[:, None] == pad_r[None, :]
    scores = jnp.einsum(
        "qhd,khd->hqk", q_blk, k_blk, preferred_element_type=jnp.float32
    ) * head ** (-0.5)
    scores = jnp.where(same[None], scores, -jnp.inf)
    top = jnp.max(scores, axis=2, keepdims=True)
    expo = jnp.exp(scores - top)
    weights = (expo / jnp.sum(expo, axis=2, keepdims=True)).astype(jnp.bfloat16)
    mixed = jnp.einsum("hqk,khd->qhd", weights, v_blk, preferred_element_type=jnp.float32)
    outputs = mixed.reshape(block, heads * head)
    return outputs


def exchange(value, axis, pairs):
    return lax.ppermute(value, axis, pairs)


def ring_gather(value, axis, n):
    rel = [None] * n
    rel[0] = value
    cw = value
    ccw = value
    for s in range(1, n // 2 + 1):
        cw = exchange(cw, axis, [(i, (i + 1) % n) for i in range(n)])
        rel[(n - s) % n] = cw
        if s < n - s:
            ccw = exchange(ccw, axis, [(i, (i - 1) % n) for i in range(n)])
            rel[s] = ccw
    return jnp.stack(rel)


def doubling_sources(n):
    return n > 1 and (n & (n - 1)) == 0


def shards(tokens, gain, qkv_weight, adapter_in, adapter_out, request_of, adapter_of, block_row):
    width = tokens.shape[1]
    rank2 = adapter_in.shape[2]
    rank = rank2 // 2
    heads_width = qkv_weight.shape[2]
    n_tp = lax.axis_size("tp")
    n_y, n_z, n_c = lax.axis_size("ry"), lax.axis_size("rz"), lax.axis_size("rc")
    split = lax.axis_index("tp")
    my_y, my_z, my_c = lax.axis_index("ry"), lax.axis_index("rz"), lax.axis_index("rc")

    request_entry = request_of[0]
    adapters = adapter_of[0]
    count = adapters.shape[0]
    rows = request_entry.shape[0]
    onehot = request_entry[:, None] == jnp.arange(count, dtype=jnp.int32)[None, :]
    live = request_entry < count

    if doubling_sources(n_tp):
        pieces, sources = [tokens], [split]
        k = 1
        while k < n_tp:
            got = exchange(jnp.stack(pieces), "tp", [(i, i ^ k) for i in range(n_tp)])
            pieces = pieces + [got[j] for j in range(got.shape[0])]
            sources = sources + [src ^ k for src in sources]
            k *= 2
    else:
        pieces, sources = [tokens], [split]
        for s in range(1, n_tp):
            pieces.append(exchange(tokens, "tp", [(i, (i + s) % n_tp) for i in range(n_tp)]))
            sources.append((split - s) % n_tp)

    n_in = adapter_in.shape[1]
    lane_w = 2 * heads_width
    down_t = adapter_in[0].T
    up_rows = adapter_out[0].reshape(2 * rank // 2, lane_w)
    packed = jnp.concatenate([down_t, up_rows], axis=0)
    per = packed.shape[0]
    if n_c > 1:
        partner = exchange(adapters, "rc", [(i, (i + 1) % n_c) for i in range(n_c)])
    every = lax.all_to_all(
        jnp.broadcast_to(packed[None], (n_z,) + packed.shape).reshape(n_z * per, lane_w),
        "rz", split_axis=0, concat_axis=0, tiled=True,
    )
    every = lax.all_gather(every, "ry", axis=0, tiled=True).reshape(n_y * n_z, per, lane_w)

    def place(ads):
        a_c = ads % n_c
        a_z = (ads // n_c) % n_z
        a_y = ads // (n_c * n_z)
        return a_y * n_z + a_z, a_c

    n_held = n_y * n_z
    table = every.reshape(n_held, per * lane_w)

    def pick(places):
        hot = (places[:, None] == jnp.arange(n_held, dtype=jnp.int32)[None, :]).astype(jnp.bfloat16)
        got = jnp.dot(hot, table, preferred_element_type=jnp.float32)
        return got.astype(jnp.bfloat16).reshape(places.shape[0], per, lane_w)

    here, a_c = place(adapters)
    if n_c > 1:
        there, _ = place(partner)
        for_partner = pick(there)
        table, for_partner = lax.optimization_barrier((table, for_partner))
        sent = exchange(for_partner, "rc", [(i, (i - 1) % n_c) for i in range(n_c)])
        sel = pick(here)
        sel = jnp.where((a_c == my_c)[:, None, None], sel, sent)
    else:
        sel = pick(here)
    sel_in = sel[:, :rank2]
    sel_out = sel[:, rank2:].reshape(count, 2, rank // 2, lane_w)

    wide = [p.astype(jnp.float32) for p in pieces]
    power = sum(jnp.sum(w * w, axis=1, keepdims=True) for w in wide) / (width * n_tp)
    scale = lax.rsqrt(power + norm_eps)
    normed = jnp.zeros((rows, width * n_tp), jnp.bfloat16)
    own = None
    for s, (w, src) in enumerate(zip(wide, sources)):
        g = lax.dynamic_slice_in_dim(gain, src * width, width)
        piece = (w * scale * g).astype(jnp.bfloat16)
        if s == 0:
            own = piece
        normed = lax.dynamic_update_slice_in_dim(normed, piece, src * width, 1)

    part = jnp.einsum("td,rkd->trk", own, sel_in, preferred_element_type=jnp.float32)
    part = jnp.sum(jnp.where(onehot[:, :, None], part, 0.0), axis=1)
    if doubling_sources(n_tp):
        total = part
        k = 1
        while k < n_tp:
            total = total + exchange(total, "tp", [(i, i ^ k) for i in range(n_tp)])
            k *= 2
    else:
        total = part
        for s in range(1, n_tp):
            total = total + exchange(part, "tp", [(i, (i + s) % n_tp) for i in range(n_tp)])
    low = total.astype(jnp.bfloat16)

    zero = jnp.zeros((), jnp.bfloat16)
    low_q = jnp.where(onehot[:, :, None], low[:, None, :rank], zero).reshape(rows, count * rank)
    low_v = jnp.where(onehot[:, :, None], low[:, None, rank:], zero).reshape(rows, count * rank)
    def up(low_m, m):
        got = None
        for h in range(2):
            lhs = low_m.reshape(rows, count, rank // 2, 2)[..., h].reshape(rows, count * rank // 2)
            rhs = sel_out[:, m, :, h * heads_width:(h + 1) * heads_width].reshape(count * rank // 2, heads_width)
            term = jnp.dot(lhs, rhs, preferred_element_type=jnp.float32)
            got = term if got is None else got + term
        return got

    delta_q = up(low_q, 0)
    delta_v = up(low_v, 1)
    delta_q = lax.reduce_precision(adapter_scale * delta_q, exponent_bits=8, mantissa_bits=7)
    delta_v = lax.reduce_precision(adapter_scale * delta_v, exponent_bits=8, mantissa_bits=7)

    base = jnp.einsum("td,jde->jte", normed, qkv_weight, preferred_element_type=jnp.float32)
    query = (base[0] + delta_q).astype(jnp.bfloat16)
    keys = base[1].astype(jnp.bfloat16)
    value = (base[2] + delta_v).astype(jnp.bfloat16)
    mixed = attend(query, keys, value, request_entry, heads_width // HEAD, HEAD)
    return jnp.where(live[:, None], mixed, 0.0).astype(jnp.bfloat16)


def torus_mesh(mesh):
    devs = mesh.devices
    n_req, n_tp = devs.shape
    col = devs[:, 0]
    try:
        n_y = len({d.coords[1] for d in col})
        n_z = len({d.coords[2] for d in col})
        n_c = len({d.core_on_chip for d in col})
    except AttributeError:
        n_y, n_z, n_c = n_req, 1, 1
    if n_y * n_z * n_c != n_req:
        n_y, n_z, n_c = n_req, 1, 1
    return Mesh(np.asarray(devs).reshape(n_y, n_z, n_c, n_tp), ("ry", "rz", "rc", "tp"))


def solution(mesh):
    grid = torus_mesh(mesh)
    req = ("ry", "rz", "rc")
    in_specs = (
        P(req, "tp"),
        P(),
        P(None, None, "tp"),
        P(req, "tp", None),
        P(req, None, None, "tp"),
        P(req, None),
        P(req, None),
        P(req, None),
    )
    out_specs = P(req, "tp")
    return jax.shard_map(shards, mesh=grid, in_specs=in_specs, out_specs=out_specs, check_vma=False)
```

```python
import jax
import jax.numpy as jnp
import numpy as np
from jax import lax
from jax.sharding import Mesh, PartitionSpec as P

HEAD = 64
LMAX = 16
LANES = 128


adapter_scale = 2.0
norm_eps = 1e-06


def attend(query, keys, value, request_entry, heads, head):
    rows = query.shape[0]
    block = min(512, rows)
    margin = LMAX
    pad_k = jnp.pad(keys, ((margin, margin), (0, 0)))
    pad_v = jnp.pad(value, ((margin, margin), (0, 0)))
    pad_r = jnp.pad(request_entry, (margin, margin), constant_values=-1)
    span = block + 2 * margin
    q_blk = query.reshape(block, heads, head)
    k_blk = pad_k.reshape(span, heads, head)
    v_blk = pad_v.reshape(span, heads, head)
    same = request_entry[:, None] == pad_r[None, :]
    scores = jnp.einsum(
        "qhd,khd->hqk", q_blk, k_blk, preferred_element_type=jnp.float32
    ) * head ** (-0.5)
    scores = jnp.where(same[None], scores, -jnp.inf)
    top = jnp.max(scores, axis=2, keepdims=True)
    expo = jnp.exp(scores - top)
    weights = (expo / jnp.sum(expo, axis=2, keepdims=True)).astype(jnp.bfloat16)
    mixed = jnp.einsum("hqk,khd->qhd", weights, v_blk, preferred_element_type=jnp.float32)
    outputs = mixed.reshape(block, heads * head)
    return outputs


def exchange(value, axis, pairs):
    return lax.ppermute(value, axis, pairs)


def ring_gather(value, axis, n):
    rel = [None] * n
    rel[0] = value
    cw = value
    ccw = value
    for s in range(1, n // 2 + 1):
        cw = exchange(cw, axis, [(i, (i + 1) % n) for i in range(n)])
        rel[(n - s) % n] = cw
        if s < n - s:
            ccw = exchange(ccw, axis, [(i, (i - 1) % n) for i in range(n)])
            rel[s] = ccw
    return jnp.stack(rel)


def doubling_sources(n):
    return n > 1 and (n & (n - 1)) == 0


def shards(tokens, gain, qkv_weight, adapter_in, adapter_out, request_of, adapter_of, block_row):
    width = tokens.shape[1]
    rank2 = adapter_in.shape[2]
    rank = rank2 // 2
    heads_width = qkv_weight.shape[2]
    n_tp = lax.axis_size("tp")
    n_y, n_z, n_c = lax.axis_size("ry"), lax.axis_size("rz"), lax.axis_size("rc")
    split = lax.axis_index("tp")
    my_y, my_z, my_c = lax.axis_index("ry"), lax.axis_index("rz"), lax.axis_index("rc")

    request_entry = request_of[0]
    adapters = adapter_of[0]
    count = adapters.shape[0]
    rows = request_entry.shape[0]
    onehot = request_entry[:, None] == jnp.arange(count, dtype=jnp.int32)[None, :]
    live = request_entry < count

    if doubling_sources(n_tp):
        pieces, sources = [tokens], [split]
        k = 1
        while k < n_tp:
            got = exchange(jnp.stack(pieces), "tp", [(i, i ^ k) for i in range(n_tp)])
            pieces = pieces + [got[j] for j in range(got.shape[0])]
            sources = sources + [src ^ k for src in sources]
            k *= 2
    else:
        pieces, sources = [tokens], [split]
        for s in range(1, n_tp):
            pieces.append(exchange(tokens, "tp", [(i, (i + s) % n_tp) for i in range(n_tp)]))
            sources.append((split - s) % n_tp)

    n_in = adapter_in.shape[1]
    lane_w = 2 * heads_width
    down_t = adapter_in[0].T
    up_rows = adapter_out[0].reshape(2 * rank // 2, lane_w)
    packed = jnp.concatenate([down_t, up_rows], axis=0)
    per = packed.shape[0]
    if n_c > 1:
        partner = exchange(adapters, "rc", [(i, (i + 1) % n_c) for i in range(n_c)])
    every = lax.all_to_all(
        jnp.broadcast_to(packed[None], (n_z,) + packed.shape).reshape(n_z * per, lane_w),
        "rz", split_axis=0, concat_axis=0, tiled=True,
    )
    every = lax.all_to_all(
        jnp.broadcast_to(every[None], (n_y,) + every.shape).reshape(n_y * n_z * per, lane_w),
        "ry", split_axis=0, concat_axis=0, tiled=True,
    ).reshape(n_y * n_z, per, lane_w)

    def place(ads):
        a_c = ads % n_c
        a_z = (ads // n_c) % n_z
        a_y = ads // (n_c * n_z)
        return a_y * n_z + a_z, a_c

    n_held = n_y * n_z
    table = every

    def pick(places):
        hot = (places[:, None] == jnp.arange(n_held, dtype=jnp.int32)[None, :]).astype(jnp.bfloat16)
        got = jnp.einsum("ra,apl->rpl", hot, table, preferred_element_type=jnp.float32)
        return got.astype(jnp.bfloat16)

    here, a_c = place(adapters)
    if n_c > 1:
        there, _ = place(partner)
        for_partner = pick(there)
        table, for_partner = lax.optimization_barrier((table, for_partner))
        sent = exchange(for_partner, "rc", [(i, (i - 1) % n_c) for i in range(n_c)])
        sel = pick(here)
        sel = jnp.where((a_c == my_c)[:, None, None], sel, sent)
    else:
        sel = pick(here)
    sel_in = sel[:, :rank2]
    sel_out = sel[:, rank2:].reshape(count, 2, rank // 2, lane_w)

    wide = [p.astype(jnp.float32) for p in pieces]
    power = sum(jnp.sum(w * w, axis=1, keepdims=True) for w in wide) / (width * n_tp)
    scale = lax.rsqrt(power + norm_eps)
    normed = jnp.zeros((rows, width * n_tp), jnp.bfloat16)
    own = None
    for s, (w, src) in enumerate(zip(wide, sources)):
        g = lax.dynamic_slice_in_dim(gain, src * width, width)
        piece = (w * scale * g).astype(jnp.bfloat16)
        if s == 0:
            own = piece
        normed = lax.dynamic_update_slice_in_dim(normed, piece, src * width, 1)

    part = jnp.einsum("td,rkd->trk", own, sel_in, preferred_element_type=jnp.float32)
    part = jnp.sum(jnp.where(onehot[:, :, None], part, 0.0), axis=1)
    if doubling_sources(n_tp):
        total = part
        k = 1
        while k < n_tp:
            total = total + exchange(total, "tp", [(i, i ^ k) for i in range(n_tp)])
            k *= 2
    else:
        total = part
        for s in range(1, n_tp):
            total = total + exchange(part, "tp", [(i, (i + s) % n_tp) for i in range(n_tp)])
    low = total.astype(jnp.bfloat16)

    zero = jnp.zeros((), jnp.bfloat16)
    low_q = jnp.where(onehot[:, :, None], low[:, None, :rank], zero).reshape(rows, count * rank)
    low_v = jnp.where(onehot[:, :, None], low[:, None, rank:], zero).reshape(rows, count * rank)
    def up(low_m, m):
        got = None
        for h in range(2):
            lhs = low_m.reshape(rows, count, rank // 2, 2)[..., h].reshape(rows, count * rank // 2)
            rhs = sel_out[:, m, :, h * heads_width:(h + 1) * heads_width].reshape(count * rank // 2, heads_width)
            term = jnp.dot(lhs, rhs, preferred_element_type=jnp.float32)
            got = term if got is None else got + term
        return got

    delta_q = up(low_q, 0)
    delta_v = up(low_v, 1)
    delta_q = lax.reduce_precision(adapter_scale * delta_q, exponent_bits=8, mantissa_bits=7)
    delta_v = lax.reduce_precision(adapter_scale * delta_v, exponent_bits=8, mantissa_bits=7)

    base = jnp.einsum("td,jde->jte", normed, qkv_weight, preferred_element_type=jnp.float32)
    query = (base[0] + delta_q).astype(jnp.bfloat16)
    keys = base[1].astype(jnp.bfloat16)
    value = (base[2] + delta_v).astype(jnp.bfloat16)
    mixed = attend(query, keys, value, request_entry, heads_width // HEAD, HEAD)
    return jnp.where(live[:, None], mixed, 0.0).astype(jnp.bfloat16)


def torus_mesh(mesh):
    devs = mesh.devices
    n_req, n_tp = devs.shape
    col = devs[:, 0]
    try:
        n_y = len({d.coords[1] for d in col})
        n_z = len({d.coords[2] for d in col})
        n_c = len({d.core_on_chip for d in col})
    except AttributeError:
        n_y, n_z, n_c = n_req, 1, 1
    if n_y * n_z * n_c != n_req:
        n_y, n_z, n_c = n_req, 1, 1
    return Mesh(np.asarray(devs).reshape(n_y, n_z, n_c, n_tp), ("ry", "rz", "rc", "tp"))


def solution(mesh):
    grid = torus_mesh(mesh)
    req = ("ry", "rz", "rc")
    in_specs = (
        P(req, "tp"),
        P(),
        P(None, None, "tp"),
        P(req, "tp", None),
        P(req, None, None, "tp"),
        P(req, None),
        P(req, None),
        P(req, None),
    )
    out_specs = P(req, "tp")
    return jax.shard_map(shards, mesh=grid, in_specs=in_specs, out_specs=out_specs, check_vma=False)
```

```python
import jax
import jax.numpy as jnp
import numpy as np
from jax import lax
from jax.experimental import pallas as pl
from jax.sharding import Mesh, PartitionSpec as P

HEAD = 64
LMAX = 16
LANES = 128


adapter_scale = 2.0
norm_eps = 1e-06


def attend(query, keys, value, request_entry, heads, head):
    rows = query.shape[0]
    block = min(512, rows)
    margin = LMAX
    pad_k = jnp.pad(keys, ((margin, margin), (0, 0)))
    pad_v = jnp.pad(value, ((margin, margin), (0, 0)))
    pad_r = jnp.pad(request_entry, (margin, margin), constant_values=-1)
    span = block + 2 * margin
    q_blk = query.reshape(block, heads, head)
    k_blk = pad_k.reshape(span, heads, head)
    v_blk = pad_v.reshape(span, heads, head)
    same = request_entry[:, None] == pad_r[None, :]
    scores = jnp.einsum(
        "qhd,khd->hqk", q_blk, k_blk, preferred_element_type=jnp.float32
    ) * head ** (-0.5)
    scores = jnp.where(same[None], scores, -jnp.inf)
    top = jnp.max(scores, axis=2, keepdims=True)
    expo = jnp.exp(scores - top)
    weights = (expo / jnp.sum(expo, axis=2, keepdims=True)).astype(jnp.bfloat16)
    mixed = jnp.einsum("hqk,khd->qhd", weights, v_blk, preferred_element_type=jnp.float32)
    outputs = mixed.reshape(block, heads * head)
    return outputs


def attend_kernel(query, keys, value, request_entry, heads, head, count, interpret=False):
    rows, cols = query.shape

    def body(q_ref, k_ref, v_ref, rc_ref, rr_ref, o_ref):
        same = rc_ref[...] == rr_ref[...]
        live = rc_ref[...] < count
        for h in range(heads):
            sl = slice(h * head, (h + 1) * head)
            scores = lax.dot_general(
                q_ref[:, sl], k_ref[:, sl], (((1,), (1,)), ((), ())),
                preferred_element_type=jnp.float32,
            ) * head ** (-0.5)
            scores = jnp.where(same, scores, -jnp.inf)
            top = jnp.max(scores, axis=1, keepdims=True)
            expo = jnp.exp(scores - top)
            weights = (expo / jnp.sum(expo, axis=1, keepdims=True)).astype(jnp.bfloat16)
            mixed = jnp.dot(weights, v_ref[:, sl], preferred_element_type=jnp.float32)
            o_ref[:, sl] = jnp.where(live, mixed, 0.0).astype(jnp.bfloat16)

    return pl.pallas_call(
        body,
        out_shape=jax.ShapeDtypeStruct((rows, cols), jnp.bfloat16),
        interpret=interpret,
    )(query, keys, value, request_entry.reshape(rows, 1), request_entry.reshape(1, rows))


def exchange(value, axis, pairs):
    return lax.ppermute(value, axis, pairs)


def ring_gather(value, axis, n):
    rel = [None] * n
    rel[0] = value
    cw = value
    ccw = value
    for s in range(1, n // 2 + 1):
        cw = exchange(cw, axis, [(i, (i + 1) % n) for i in range(n)])
        rel[(n - s) % n] = cw
        if s < n - s:
            ccw = exchange(ccw, axis, [(i, (i - 1) % n) for i in range(n)])
            rel[s] = ccw
    return jnp.stack(rel)


def doubling_sources(n):
    return n > 1 and (n & (n - 1)) == 0


def shards(tokens, gain, qkv_weight, adapter_in, adapter_out, request_of, adapter_of, block_row):
    width = tokens.shape[1]
    rank2 = adapter_in.shape[2]
    rank = rank2 // 2
    heads_width = qkv_weight.shape[2]
    n_tp = lax.axis_size("tp")
    n_y, n_z, n_c = lax.axis_size("ry"), lax.axis_size("rz"), lax.axis_size("rc")
    split = lax.axis_index("tp")
    my_y, my_z, my_c = lax.axis_index("ry"), lax.axis_index("rz"), lax.axis_index("rc")

    request_entry = request_of[0]
    adapters = adapter_of[0]
    count = adapters.shape[0]
    rows = request_entry.shape[0]
    onehot = request_entry[:, None] == jnp.arange(count, dtype=jnp.int32)[None, :]
    live = request_entry < count

    if doubling_sources(n_tp):
        pieces, sources = [tokens], [split]
        k = 1
        while k < n_tp:
            got = exchange(jnp.stack(pieces), "tp", [(i, i ^ k) for i in range(n_tp)])
            pieces = pieces + [got[j] for j in range(got.shape[0])]
            sources = sources + [src ^ k for src in sources]
            k *= 2
    else:
        pieces, sources = [tokens], [split]
        for s in range(1, n_tp):
            pieces.append(exchange(tokens, "tp", [(i, (i + s) % n_tp) for i in range(n_tp)]))
            sources.append((split - s) % n_tp)

    n_in = adapter_in.shape[1]
    lane_w = 2 * heads_width
    down_t = adapter_in[0].T
    up_rows = adapter_out[0].reshape(2 * rank // 2, lane_w)
    packed = jnp.concatenate([down_t, up_rows], axis=0)
    per = packed.shape[0]
    if n_c > 1:
        partner = exchange(adapters, "rc", [(i, (i + 1) % n_c) for i in range(n_c)])
    every = lax.all_to_all(
        jnp.broadcast_to(packed[None], (n_z,) + packed.shape).reshape(n_z * per, lane_w),
        "rz", split_axis=0, concat_axis=0, tiled=True,
    )
    every = lax.all_gather(every, "ry", axis=0, tiled=True).reshape(n_y * n_z, per, lane_w)

    def place(ads):
        a_c = ads % n_c
        a_z = (ads // n_c) % n_z
        a_y = ads // (n_c * n_z)
        return a_y * n_z + a_z, a_c

    n_held = n_y * n_z
    table = every.reshape(n_held, per * lane_w)

    def pick(places):
        hot = (places[:, None] == jnp.arange(n_held, dtype=jnp.int32)[None, :]).astype(jnp.bfloat16)
        got = jnp.dot(hot, table, preferred_element_type=jnp.float32)
        return got.astype(jnp.bfloat16).reshape(places.shape[0], per, lane_w)

    here, a_c = place(adapters)
    if n_c > 1:
        there, _ = place(partner)
        for_partner = pick(there)
        table, for_partner = lax.optimization_barrier((table, for_partner))
        sent = exchange(for_partner, "rc", [(i, (i - 1) % n_c) for i in range(n_c)])
        sel = pick(here)
        sel = jnp.where((a_c == my_c)[:, None, None], sel, sent)
    else:
        sel = pick(here)
    sel_in = sel[:, :rank2]
    sel_out = sel[:, rank2:].reshape(count, 2, rank // 2, lane_w)

    wide = [p.astype(jnp.float32) for p in pieces]
    power = sum(jnp.sum(w * w, axis=1, keepdims=True) for w in wide) / (width * n_tp)
    scale = lax.rsqrt(power + norm_eps)
    normed = jnp.zeros((rows, width * n_tp), jnp.bfloat16)
    own = None
    for s, (w, src) in enumerate(zip(wide, sources)):
        g = lax.dynamic_slice_in_dim(gain, src * width, width)
        piece = (w * scale * g).astype(jnp.bfloat16)
        if s == 0:
            own = piece
        normed = lax.dynamic_update_slice_in_dim(normed, piece, src * width, 1)

    part = jnp.einsum("td,rkd->trk", own, sel_in, preferred_element_type=jnp.float32)
    part = jnp.sum(jnp.where(onehot[:, :, None], part, 0.0), axis=1)
    if doubling_sources(n_tp):
        total = part
        k = 1
        while k < n_tp:
            total = total + exchange(total, "tp", [(i, i ^ k) for i in range(n_tp)])
            k *= 2
    else:
        total = part
        for s in range(1, n_tp):
            total = total + exchange(part, "tp", [(i, (i + s) % n_tp) for i in range(n_tp)])
    low = total.astype(jnp.bfloat16)

    zero = jnp.zeros((), jnp.bfloat16)
    low_q = jnp.where(onehot[:, :, None], low[:, None, :rank], zero).reshape(rows, count * rank)
    low_v = jnp.where(onehot[:, :, None], low[:, None, rank:], zero).reshape(rows, count * rank)
    def up(low_m, m):
        got = None
        for h in range(2):
            lhs = low_m.reshape(rows, count, rank // 2, 2)[..., h].reshape(rows, count * rank // 2)
            rhs = sel_out[:, m, :, h * heads_width:(h + 1) * heads_width].reshape(count * rank // 2, heads_width)
            term = jnp.dot(lhs, rhs, preferred_element_type=jnp.float32)
            got = term if got is None else got + term
        return got

    delta_q = up(low_q, 0)
    delta_v = up(low_v, 1)
    delta_q = lax.reduce_precision(adapter_scale * delta_q, exponent_bits=8, mantissa_bits=7)
    delta_v = lax.reduce_precision(adapter_scale * delta_v, exponent_bits=8, mantissa_bits=7)

    base = jnp.einsum("td,jde->jte", normed, qkv_weight, preferred_element_type=jnp.float32)
    query = (base[0] + delta_q).astype(jnp.bfloat16)
    keys = base[1].astype(jnp.bfloat16)
    value = (base[2] + delta_v).astype(jnp.bfloat16)
    return attend_kernel(query, keys, value, request_entry, heads_width // HEAD, HEAD, count)


def torus_mesh(mesh):
    devs = mesh.devices
    n_req, n_tp = devs.shape
    col = devs[:, 0]
    try:
        n_y = len({d.coords[1] for d in col})
        n_z = len({d.coords[2] for d in col})
        n_c = len({d.core_on_chip for d in col})
    except AttributeError:
        n_y, n_z, n_c = n_req, 1, 1
    if n_y * n_z * n_c != n_req:
        n_y, n_z, n_c = n_req, 1, 1
    return Mesh(np.asarray(devs).reshape(n_y, n_z, n_c, n_tp), ("ry", "rz", "rc", "tp"))


def solution(mesh):
    grid = torus_mesh(mesh)
    req = ("ry", "rz", "rc")
    in_specs = (
        P(req, "tp"),
        P(),
        P(None, None, "tp"),
        P(req, "tp", None),
        P(req, None, None, "tp"),
        P(req, None),
        P(req, None),
        P(req, None),
    )
    out_specs = P(req, "tp")
    return jax.shard_map(shards, mesh=grid, in_specs=in_specs, out_specs=out_specs, check_vma=False)
```

```python
import jax
import jax.numpy as jnp
import numpy as np
from jax import lax
from jax.experimental import pallas as pl
from jax.experimental.pallas import tpu as pltpu
from jax.sharding import Mesh, PartitionSpec as P

HEAD = 64
LMAX = 16
LANES = 128


adapter_scale = 2.0
norm_eps = 1e-06


def attend(query, keys, value, request_entry, heads, head):
    rows = query.shape[0]
    block = min(512, rows)
    margin = LMAX
    pad_k = jnp.pad(keys, ((margin, margin), (0, 0)))
    pad_v = jnp.pad(value, ((margin, margin), (0, 0)))
    pad_r = jnp.pad(request_entry, (margin, margin), constant_values=-1)
    span = block + 2 * margin
    q_blk = query.reshape(block, heads, head)
    k_blk = pad_k.reshape(span, heads, head)
    v_blk = pad_v.reshape(span, heads, head)
    same = request_entry[:, None] == pad_r[None, :]
    scores = jnp.einsum(
        "qhd,khd->hqk", q_blk, k_blk, preferred_element_type=jnp.float32
    ) * head ** (-0.5)
    scores = jnp.where(same[None], scores, -jnp.inf)
    top = jnp.max(scores, axis=2, keepdims=True)
    expo = jnp.exp(scores - top)
    weights = (expo / jnp.sum(expo, axis=2, keepdims=True)).astype(jnp.bfloat16)
    mixed = jnp.einsum("hqk,khd->qhd", weights, v_blk, preferred_element_type=jnp.float32)
    outputs = mixed.reshape(block, heads * head)
    return outputs


def attend_kernel(query, keys, value, request_entry, heads, head, count, interpret=False):
    rows, cols = query.shape

    def body(q_ref, k_ref, v_ref, rc_ref, rr_ref, o_ref):
        same = rc_ref[...] == rr_ref[...]
        live = rc_ref[...] < count
        for h in range(heads):
            sl = slice(h * head, (h + 1) * head)
            scores = lax.dot_general(
                q_ref[:, sl], k_ref[:, sl], (((1,), (1,)), ((), ())),
                preferred_element_type=jnp.float32,
            ) * head ** (-0.5)
            scores = jnp.where(same, scores, -jnp.inf)
            top = jnp.max(scores, axis=1, keepdims=True)
            expo = jnp.exp(scores - top)
            weights = (expo / jnp.sum(expo, axis=1, keepdims=True)).astype(jnp.bfloat16)
            mixed = jnp.dot(weights, v_ref[:, sl], preferred_element_type=jnp.float32)
            o_ref[:, sl] = jnp.where(live, mixed, 0.0).astype(jnp.bfloat16)

    return pl.pallas_call(
        body,
        out_shape=jax.ShapeDtypeStruct((rows, cols), jnp.bfloat16),
        interpret=interpret,
    )(query, keys, value, request_entry.reshape(rows, 1), request_entry.reshape(1, rows))


def slab_gather(table, places, interpret=False):
    n_out = places.shape[0]

    def body(idx_ref, tab_ref, out_ref, sems):
        copies = [
            pltpu.make_async_copy(tab_ref.at[idx_ref[r]], out_ref.at[r], sems.at[r])
            for r in range(n_out)
        ]
        for c in copies:
            c.start()
        for c in copies:
            c.wait()

    return pl.pallas_call(
        body,
        out_shape=jax.ShapeDtypeStruct((n_out,) + table.shape[1:], table.dtype),
        grid_spec=pltpu.PrefetchScalarGridSpec(
            num_scalar_prefetch=1,
            grid=(1,),
            in_specs=[pl.BlockSpec(memory_space=pl.ANY)],
            out_specs=pl.BlockSpec(memory_space=pl.ANY),
            scratch_shapes=[pltpu.SemaphoreType.DMA((n_out,))],
        ),
        interpret=interpret,
    )(places, table)


def exchange(value, axis, pairs):
    return lax.ppermute(value, axis, pairs)


def ring_gather(value, axis, n):
    rel = [None] * n
    rel[0] = value
    cw = value
    ccw = value
    for s in range(1, n // 2 + 1):
        cw = exchange(cw, axis, [(i, (i + 1) % n) for i in range(n)])
        rel[(n - s) % n] = cw
        if s < n - s:
            ccw = exchange(ccw, axis, [(i, (i - 1) % n) for i in range(n)])
            rel[s] = ccw
    return jnp.stack(rel)


def doubling_sources(n):
    return n > 1 and (n & (n - 1)) == 0


def shards(tokens, gain, qkv_weight, adapter_in, adapter_out, request_of, adapter_of, block_row):
    width = tokens.shape[1]
    rank2 = adapter_in.shape[2]
    rank = rank2 // 2
    heads_width = qkv_weight.shape[2]
    n_tp = lax.axis_size("tp")
    n_y, n_z, n_c = lax.axis_size("ry"), lax.axis_size("rz"), lax.axis_size("rc")
    split = lax.axis_index("tp")
    my_y, my_z, my_c = lax.axis_index("ry"), lax.axis_index("rz"), lax.axis_index("rc")

    request_entry = request_of[0]
    adapters = adapter_of[0]
    count = adapters.shape[0]
    rows = request_entry.shape[0]
    onehot = request_entry[:, None] == jnp.arange(count, dtype=jnp.int32)[None, :]
    live = request_entry < count

    if doubling_sources(n_tp):
        pieces, sources = [tokens], [split]
        k = 1
        while k < n_tp:
            got = exchange(jnp.stack(pieces), "tp", [(i, i ^ k) for i in range(n_tp)])
            pieces = pieces + [got[j] for j in range(got.shape[0])]
            sources = sources + [src ^ k for src in sources]
            k *= 2
    else:
        pieces, sources = [tokens], [split]
        for s in range(1, n_tp):
            pieces.append(exchange(tokens, "tp", [(i, (i + s) % n_tp) for i in range(n_tp)]))
            sources.append((split - s) % n_tp)

    n_in = adapter_in.shape[1]
    lane_w = 2 * heads_width
    down_t = adapter_in[0].T
    up_rows = adapter_out[0].reshape(2 * rank // 2, lane_w)
    packed = jnp.concatenate([down_t, up_rows], axis=0)
    per = packed.shape[0]
    if n_c > 1:
        partner = exchange(adapters, "rc", [(i, (i + 1) % n_c) for i in range(n_c)])
    every = lax.all_to_all(
        jnp.broadcast_to(packed[None], (n_z,) + packed.shape).reshape(n_z * per, lane_w),
        "rz", split_axis=0, concat_axis=0, tiled=True,
    )
    every = lax.all_gather(every, "ry", axis=0, tiled=True).reshape(n_y * n_z, per, lane_w)

    def place(ads):
        a_c = ads % n_c
        a_z = (ads // n_c) % n_z
        a_y = ads // (n_c * n_z)
        return a_y * n_z + a_z, a_c

    n_held = n_y * n_z
    table = every

    def pick(places):
        return slab_gather(table, places)

    here, a_c = place(adapters)
    if n_c > 1:
        there, _ = place(partner)
        for_partner = pick(there)
        table, for_partner = lax.optimization_barrier((table, for_partner))
        sent = exchange(for_partner, "rc", [(i, (i - 1) % n_c) for i in range(n_c)])
        sel = pick(here)
        sel = jnp.where((a_c == my_c)[:, None, None], sel, sent)
    else:
        sel = pick(here)
    sel_in = sel[:, :rank2]
    sel_out = sel[:, rank2:].reshape(count, 2, rank // 2, lane_w)

    wide = [p.astype(jnp.float32) for p in pieces]
    power = sum(jnp.sum(w * w, axis=1, keepdims=True) for w in wide) / (width * n_tp)
    scale = lax.rsqrt(power + norm_eps)
    normed = jnp.zeros((rows, width * n_tp), jnp.bfloat16)
    own = None
    for s, (w, src) in enumerate(zip(wide, sources)):
        g = lax.dynamic_slice_in_dim(gain, src * width, width)
        piece = (w * scale * g).astype(jnp.bfloat16)
        if s == 0:
            own = piece
        normed = lax.dynamic_update_slice_in_dim(normed, piece, src * width, 1)

    part = jnp.einsum("td,rkd->trk", own, sel_in, preferred_element_type=jnp.float32)
    part = jnp.sum(jnp.where(onehot[:, :, None], part, 0.0), axis=1)
    if doubling_sources(n_tp):
        total = part
        k = 1
        while k < n_tp:
            total = total + exchange(total, "tp", [(i, i ^ k) for i in range(n_tp)])
            k *= 2
    else:
        total = part
        for s in range(1, n_tp):
            total = total + exchange(part, "tp", [(i, (i + s) % n_tp) for i in range(n_tp)])
    low = total.astype(jnp.bfloat16)

    zero = jnp.zeros((), jnp.bfloat16)
    low_q = jnp.where(onehot[:, :, None], low[:, None, :rank], zero).reshape(rows, count * rank)
    low_v = jnp.where(onehot[:, :, None], low[:, None, rank:], zero).reshape(rows, count * rank)
    def up(low_m, m):
        got = None
        for h in range(2):
            lhs = low_m.reshape(rows, count, rank // 2, 2)[..., h].reshape(rows, count * rank // 2)
            rhs = sel_out[:, m, :, h * heads_width:(h + 1) * heads_width].reshape(count * rank // 2, heads_width)
            term = jnp.dot(lhs, rhs, preferred_element_type=jnp.float32)
            got = term if got is None else got + term
        return got

    delta_q = up(low_q, 0)
    delta_v = up(low_v, 1)
    delta_q = lax.reduce_precision(adapter_scale * delta_q, exponent_bits=8, mantissa_bits=7)
    delta_v = lax.reduce_precision(adapter_scale * delta_v, exponent_bits=8, mantissa_bits=7)

    base = jnp.einsum("td,jde->jte", normed, qkv_weight, preferred_element_type=jnp.float32)
    query = (base[0] + delta_q).astype(jnp.bfloat16)
    keys = base[1].astype(jnp.bfloat16)
    value = (base[2] + delta_v).astype(jnp.bfloat16)
    return attend_kernel(query, keys, value, request_entry, heads_width // HEAD, HEAD, count)


def torus_mesh(mesh):
    devs = mesh.devices
    n_req, n_tp = devs.shape
    col = devs[:, 0]
    try:
        n_y = len({d.coords[1] for d in col})
        n_z = len({d.coords[2] for d in col})
        n_c = len({d.core_on_chip for d in col})
    except AttributeError:
        n_y, n_z, n_c = n_req, 1, 1
    if n_y * n_z * n_c != n_req:
        n_y, n_z, n_c = n_req, 1, 1
    return Mesh(np.asarray(devs).reshape(n_y, n_z, n_c, n_tp), ("ry", "rz", "rc", "tp"))


def solution(mesh):
    grid = torus_mesh(mesh)
    req = ("ry", "rz", "rc")
    in_specs = (
        P(req, "tp"),
        P(),
        P(None, None, "tp"),
        P(req, "tp", None),
        P(req, None, None, "tp"),
        P(req, None),
        P(req, None),
        P(req, None),
    )
    out_specs = P(req, "tp")
    return jax.shard_map(shards, mesh=grid, in_specs=in_specs, out_specs=out_specs, check_vma=False)
```

```python
import jax
import jax.numpy as jnp
import numpy as np
from jax import lax
from jax.experimental import pallas as pl
from jax.sharding import Mesh, PartitionSpec as P

HEAD = 64
LMAX = 16
LANES = 128


adapter_scale = 2.0
norm_eps = 1e-06


def attend(query, keys, value, request_entry, heads, head):
    rows = query.shape[0]
    block = min(512, rows)
    margin = LMAX
    pad_k = jnp.pad(keys, ((margin, margin), (0, 0)))
    pad_v = jnp.pad(value, ((margin, margin), (0, 0)))
    pad_r = jnp.pad(request_entry, (margin, margin), constant_values=-1)
    span = block + 2 * margin
    q_blk = query.reshape(block, heads, head)
    k_blk = pad_k.reshape(span, heads, head)
    v_blk = pad_v.reshape(span, heads, head)
    same = request_entry[:, None] == pad_r[None, :]
    scores = jnp.einsum(
        "qhd,khd->hqk", q_blk, k_blk, preferred_element_type=jnp.float32
    ) * head ** (-0.5)
    scores = jnp.where(same[None], scores, -jnp.inf)
    top = jnp.max(scores, axis=2, keepdims=True)
    expo = jnp.exp(scores - top)
    weights = (expo / jnp.sum(expo, axis=2, keepdims=True)).astype(jnp.bfloat16)
    mixed = jnp.einsum("hqk,khd->qhd", weights, v_blk, preferred_element_type=jnp.float32)
    outputs = mixed.reshape(block, heads * head)
    return outputs


def attend_kernel(query, keys, value, request_entry, heads, head, count, interpret=False):
    rows, cols = query.shape

    def body(q_ref, k_ref, v_ref, rc_ref, rr_ref, o_ref):
        same = rc_ref[...] == rr_ref[...]
        live = rc_ref[...] < count
        for h in range(heads):
            sl = slice(h * head, (h + 1) * head)
            scores = lax.dot_general(
                q_ref[:, sl], k_ref[:, sl], (((1,), (1,)), ((), ())),
                preferred_element_type=jnp.float32,
            ) * head ** (-0.5)
            scores = jnp.where(same, scores, -jnp.inf)
            top = jnp.max(scores, axis=1, keepdims=True)
            expo = jnp.exp(scores - top)
            weights = (expo / jnp.sum(expo, axis=1, keepdims=True)).astype(jnp.bfloat16)
            mixed = jnp.dot(weights, v_ref[:, sl], preferred_element_type=jnp.float32)
            o_ref[:, sl] = jnp.where(live, mixed, 0.0).astype(jnp.bfloat16)

    return pl.pallas_call(
        body,
        out_shape=jax.ShapeDtypeStruct((rows, cols), jnp.bfloat16),
        interpret=interpret,
    )(query, keys, value, request_entry.reshape(rows, 1), request_entry.reshape(1, rows))


def exchange(value, axis, pairs):
    return lax.ppermute(value, axis, pairs)


def ring_gather(value, axis, n):
    rel = [None] * n
    rel[0] = value
    cw = value
    ccw = value
    for s in range(1, n // 2 + 1):
        cw = exchange(cw, axis, [(i, (i + 1) % n) for i in range(n)])
        rel[(n - s) % n] = cw
        if s < n - s:
            ccw = exchange(ccw, axis, [(i, (i - 1) % n) for i in range(n)])
            rel[s] = ccw
    return jnp.stack(rel)


def doubling_sources(n):
    return n > 1 and (n & (n - 1)) == 0


def shards(tokens, gain, qkv_weight, adapter_in, adapter_out, request_of, adapter_of, block_row):
    width = tokens.shape[1]
    rank2 = adapter_in.shape[2]
    rank = rank2 // 2
    heads_width = qkv_weight.shape[2]
    n_tp = lax.axis_size("tp")
    n_y, n_z, n_c = lax.axis_size("ry"), lax.axis_size("rz"), lax.axis_size("rc")
    split = lax.axis_index("tp")
    my_y, my_z, my_c = lax.axis_index("ry"), lax.axis_index("rz"), lax.axis_index("rc")

    request_entry = request_of[0]
    adapters = adapter_of[0]
    count = adapters.shape[0]
    rows = request_entry.shape[0]
    onehot = request_entry[:, None] == jnp.arange(count, dtype=jnp.int32)[None, :]
    live = request_entry < count

    if doubling_sources(n_tp):
        pieces, sources = [tokens], [split]
        k = 1
        while k < n_tp:
            got = exchange(jnp.stack(pieces), "tp", [(i, i ^ k) for i in range(n_tp)])
            pieces = pieces + [got[j] for j in range(got.shape[0])]
            sources = sources + [src ^ k for src in sources]
            k *= 2
    else:
        pieces, sources = [tokens], [split]
        for s in range(1, n_tp):
            pieces.append(exchange(tokens, "tp", [(i, (i + s) % n_tp) for i in range(n_tp)]))
            sources.append((split - s) % n_tp)

    n_in = adapter_in.shape[1]
    lane_w = 2 * heads_width
    down_t = adapter_in[0].T
    up_rows = adapter_out[0].reshape(2 * rank // 2, lane_w)
    packed = jnp.concatenate([down_t, up_rows], axis=0)
    per = packed.shape[0]
    if n_c > 1:
        partner = exchange(adapters, "rc", [(i, (i + 1) % n_c) for i in range(n_c)])
    every = lax.all_to_all(
        jnp.broadcast_to(packed[None], (n_z,) + packed.shape).reshape(n_z * per, lane_w),
        "rz", split_axis=0, concat_axis=0, tiled=True,
    )
    every = lax.all_gather(every, "ry", axis=0, tiled=True).reshape(n_y * n_z, per, lane_w)

    def place(ads):
        a_c = ads % n_c
        a_z = (ads // n_c) % n_z
        a_y = ads // (n_c * n_z)
        return a_y * n_z + a_z, a_c

    n_held = n_y * n_z
    table = every.reshape(n_held, per * lane_w)

    def pick(places):
        hot = (places[:, None] == jnp.arange(n_held, dtype=jnp.int32)[None, :]).astype(jnp.bfloat16)
        got = jnp.dot(hot, table, preferred_element_type=jnp.float32)
        return got.astype(jnp.bfloat16).reshape(places.shape[0], per, lane_w)

    here, a_c = place(adapters)
    if n_c > 1:
        there, _ = place(partner)
        for_partner = pick(there)
        table, for_partner = lax.optimization_barrier((table, for_partner))
        sent = exchange(for_partner, "rc", [(i, (i - 1) % n_c) for i in range(n_c)])
        sel = pick(here)
        sel = jnp.where((a_c == my_c)[:, None, None], sel, sent)
    else:
        sel = pick(here)
    sel_in = sel[:, :rank2]
    sel_out = sel[:, rank2:].reshape(count, 2, rank // 2, lane_w)

    wide = [p.astype(jnp.float32) for p in pieces]
    power = sum(jnp.sum(w * w, axis=1, keepdims=True) for w in wide) / (width * n_tp)
    scale = lax.rsqrt(power + norm_eps)
    normed = jnp.zeros((rows, width * n_tp), jnp.bfloat16)
    own = None
    for s, (w, src) in enumerate(zip(wide, sources)):
        g = lax.dynamic_slice_in_dim(gain, src * width, width)
        piece = (w * scale * g).astype(jnp.bfloat16)
        if s == 0:
            own = piece
        normed = lax.dynamic_update_slice_in_dim(normed, piece, src * width, 1)

    part = jnp.einsum("td,rkd->trk", own, sel_in, preferred_element_type=jnp.float32)
    part = jnp.sum(jnp.where(onehot[:, :, None], part, 0.0), axis=1)
    partials = lax.all_to_all(
        jnp.broadcast_to(part[None], (n_tp,) + part.shape), "tp", split_axis=0, concat_axis=0, tiled=True
    )
    total = partials[0]
    for s in range(1, n_tp):
        total = total + partials[s]
    low = total.astype(jnp.bfloat16)

    zero = jnp.zeros((), jnp.bfloat16)
    low_q = jnp.where(onehot[:, :, None], low[:, None, :rank], zero).reshape(rows, count * rank)
    low_v = jnp.where(onehot[:, :, None], low[:, None, rank:], zero).reshape(rows, count * rank)
    def up(low_m, m):
        got = None
        for h in range(2):
            lhs = low_m.reshape(rows, count, rank // 2, 2)[..., h].reshape(rows, count * rank // 2)
            rhs = sel_out[:, m, :, h * heads_width:(h + 1) * heads_width].reshape(count * rank // 2, heads_width)
            term = jnp.dot(lhs, rhs, preferred_element_type=jnp.float32)
            got = term if got is None else got + term
        return got

    delta_q = up(low_q, 0)
    delta_v = up(low_v, 1)
    delta_q = lax.reduce_precision(adapter_scale * delta_q, exponent_bits=8, mantissa_bits=7)
    delta_v = lax.reduce_precision(adapter_scale * delta_v, exponent_bits=8, mantissa_bits=7)

    base = jnp.einsum("td,jde->jte", normed, qkv_weight, preferred_element_type=jnp.float32)
    query = (base[0] + delta_q).astype(jnp.bfloat16)
    keys = base[1].astype(jnp.bfloat16)
    value = (base[2] + delta_v).astype(jnp.bfloat16)
    return attend_kernel(query, keys, value, request_entry, heads_width // HEAD, HEAD, count)


def torus_mesh(mesh):
    devs = mesh.devices
    n_req, n_tp = devs.shape
    col = devs[:, 0]
    try:
        n_y = len({d.coords[1] for d in col})
        n_z = len({d.coords[2] for d in col})
        n_c = len({d.core_on_chip for d in col})
    except AttributeError:
        n_y, n_z, n_c = n_req, 1, 1
    if n_y * n_z * n_c != n_req:
        n_y, n_z, n_c = n_req, 1, 1
    return Mesh(np.asarray(devs).reshape(n_y, n_z, n_c, n_tp), ("ry", "rz", "rc", "tp"))


def solution(mesh):
    grid = torus_mesh(mesh)
    req = ("ry", "rz", "rc")
    in_specs = (
        P(req, "tp"),
        P(),
        P(None, None, "tp"),
        P(req, "tp", None),
        P(req, None, None, "tp"),
        P(req, None),
        P(req, None),
        P(req, None),
    )
    out_specs = P(req, "tp")
    return jax.shard_map(shards, mesh=grid, in_specs=in_specs, out_specs=out_specs, check_vma=False)
```

```python
import jax
import jax.numpy as jnp
import numpy as np
from jax import lax
from jax.experimental import pallas as pl
from jax.sharding import Mesh, PartitionSpec as P

HEAD = 64
LMAX = 16
LANES = 128


adapter_scale = 2.0
norm_eps = 1e-06


def attend(query, keys, value, request_entry, heads, head):
    rows = query.shape[0]
    block = min(512, rows)
    margin = LMAX
    pad_k = jnp.pad(keys, ((margin, margin), (0, 0)))
    pad_v = jnp.pad(value, ((margin, margin), (0, 0)))
    pad_r = jnp.pad(request_entry, (margin, margin), constant_values=-1)
    span = block + 2 * margin
    q_blk = query.reshape(block, heads, head)
    k_blk = pad_k.reshape(span, heads, head)
    v_blk = pad_v.reshape(span, heads, head)
    same = request_entry[:, None] == pad_r[None, :]
    scores = jnp.einsum(
        "qhd,khd->hqk", q_blk, k_blk, preferred_element_type=jnp.float32
    ) * head ** (-0.5)
    scores = jnp.where(same[None], scores, -jnp.inf)
    top = jnp.max(scores, axis=2, keepdims=True)
    expo = jnp.exp(scores - top)
    weights = (expo / jnp.sum(expo, axis=2, keepdims=True)).astype(jnp.bfloat16)
    mixed = jnp.einsum("hqk,khd->qhd", weights, v_blk, preferred_element_type=jnp.float32)
    outputs = mixed.reshape(block, heads * head)
    return outputs


def attend_kernel(query, keys, value, request_entry, heads, head, count, interpret=False):
    rows, cols = query.shape

    def body(q_ref, k_ref, v_ref, rc_ref, rr_ref, o_ref):
        same = rc_ref[...] == rr_ref[...]
        live = rc_ref[...] < count
        for h in range(heads):
            sl = slice(h * head, (h + 1) * head)
            scores = lax.dot_general(
                q_ref[:, sl], k_ref[:, sl], (((1,), (1,)), ((), ())),
                preferred_element_type=jnp.float32,
            ) * head ** (-0.5)
            scores = jnp.where(same, scores, -jnp.inf)
            top = jnp.max(scores, axis=1, keepdims=True)
            expo = jnp.exp(scores - top)
            weights = (expo / jnp.sum(expo, axis=1, keepdims=True)).astype(jnp.bfloat16)
            mixed = jnp.dot(weights, v_ref[:, sl], preferred_element_type=jnp.float32)
            o_ref[:, sl] = jnp.where(live, mixed, 0.0).astype(jnp.bfloat16)

    return pl.pallas_call(
        body,
        out_shape=jax.ShapeDtypeStruct((rows, cols), jnp.bfloat16),
        interpret=interpret,
    )(query, keys, value, request_entry.reshape(rows, 1), request_entry.reshape(1, rows))


def exchange(value, axis, pairs):
    return lax.ppermute(value, axis, pairs)


def ring_gather(value, axis, n):
    rel = [None] * n
    rel[0] = value
    cw = value
    ccw = value
    for s in range(1, n // 2 + 1):
        cw = exchange(cw, axis, [(i, (i + 1) % n) for i in range(n)])
        rel[(n - s) % n] = cw
        if s < n - s:
            ccw = exchange(ccw, axis, [(i, (i - 1) % n) for i in range(n)])
            rel[s] = ccw
    return jnp.stack(rel)


def doubling_sources(n):
    return n > 1 and (n & (n - 1)) == 0


def shards(tokens, gain, qkv_weight, adapter_in, adapter_out, request_of, adapter_of, block_row):
    width = tokens.shape[1]
    rank2 = adapter_in.shape[2]
    rank = rank2 // 2
    heads_width = qkv_weight.shape[2]
    n_tp = lax.axis_size("tp")
    n_y, n_z, n_c = lax.axis_size("ry"), lax.axis_size("rz"), lax.axis_size("rc")
    split = lax.axis_index("tp")
    my_y, my_z, my_c = lax.axis_index("ry"), lax.axis_index("rz"), lax.axis_index("rc")

    request_entry = request_of[0]
    adapters = adapter_of[0]
    count = adapters.shape[0]
    rows = request_entry.shape[0]
    onehot = request_entry[:, None] == jnp.arange(count, dtype=jnp.int32)[None, :]
    live = request_entry < count

    if doubling_sources(n_tp):
        pieces, sources = [tokens], [split]
        k = 1
        while k < n_tp:
            got = exchange(jnp.stack(pieces), "tp", [(i, i ^ k) for i in range(n_tp)])
            pieces = pieces + [got[j] for j in range(got.shape[0])]
            sources = sources + [src ^ k for src in sources]
            k *= 2
    else:
        pieces, sources = [tokens], [split]
        for s in range(1, n_tp):
            pieces.append(exchange(tokens, "tp", [(i, (i + s) % n_tp) for i in range(n_tp)]))
            sources.append((split - s) % n_tp)

    n_in = adapter_in.shape[1]
    lane_w = 2 * heads_width
    down_t = adapter_in[0].T
    up_rows = adapter_out[0].reshape(2 * rank // 2, lane_w)
    packed = jnp.concatenate([down_t, up_rows], axis=0)
    per = packed.shape[0]
    if n_c > 1:
        partner = exchange(adapters, "rc", [(i, (i + 1) % n_c) for i in range(n_c)])
    every = lax.all_to_all(
        jnp.broadcast_to(packed[None], (n_z,) + packed.shape).reshape(n_z * per, lane_w),
        "rz", split_axis=0, concat_axis=0, tiled=True,
    )
    every = lax.all_gather(every, "ry", axis=0, tiled=True).reshape(n_y * n_z, per, lane_w)

    def place(ads):
        a_c = ads % n_c
        a_z = (ads // n_c) % n_z
        a_y = ads // (n_c * n_z)
        return a_y * n_z + a_z, a_c

    n_held = n_y * n_z
    table = every.reshape(n_held, per * lane_w)

    def pick(places):
        hot = (places[:, None] == jnp.arange(n_held, dtype=jnp.int32)[None, :]).astype(jnp.bfloat16)
        got = jnp.dot(hot, table, preferred_element_type=jnp.float32)
        return got.astype(jnp.bfloat16).reshape(places.shape[0], per, lane_w)

    here, a_c = place(adapters)
    if n_c > 1:
        there, _ = place(partner)
        for_partner = pick(there)
        table, for_partner = lax.optimization_barrier((table, for_partner))
        sent = exchange(for_partner, "rc", [(i, (i - 1) % n_c) for i in range(n_c)])
        sel = pick(here)
        sel = jnp.where((a_c == my_c)[:, None, None], sel, sent)
    else:
        sel = pick(here)
    sel_in = sel[:, :rank2]
    sel_out = sel[:, rank2:].reshape(count, 2, rank // 2, lane_w)

    wide = [p.astype(jnp.float32) for p in pieces]
    power = sum(jnp.sum(w * w, axis=1, keepdims=True) for w in wide) / (width * n_tp)
    scale = lax.rsqrt(power + norm_eps)
    normed = jnp.zeros((rows, width * n_tp), jnp.bfloat16)
    own = None
    for s, (w, src) in enumerate(zip(wide, sources)):
        g = lax.dynamic_slice_in_dim(gain, src * width, width)
        piece = (w * scale * g).astype(jnp.bfloat16)
        if s == 0:
            own = piece
        normed = lax.dynamic_update_slice_in_dim(normed, piece, src * width, 1)

    part = lax.dot_general(
        own, sel_in.reshape(count * rank2, width), (((1,), (1,)), ((), ())),
        preferred_element_type=jnp.float32,
    ).reshape(rows, count, rank2)
    part = jnp.sum(jnp.where(onehot[:, :, None], part, 0.0), axis=1)
    if doubling_sources(n_tp):
        total = part
        k = 1
        while k < n_tp:
            total = total + exchange(total, "tp", [(i, i ^ k) for i in range(n_tp)])
            k *= 2
    else:
        total = part
        for s in range(1, n_tp):
            total = total + exchange(part, "tp", [(i, (i + s) % n_tp) for i in range(n_tp)])
    low = total.astype(jnp.bfloat16)

    zero = jnp.zeros((), jnp.bfloat16)
    low_q = jnp.where(onehot[:, :, None], low[:, None, :rank], zero).reshape(rows, count * rank)
    low_v = jnp.where(onehot[:, :, None], low[:, None, rank:], zero).reshape(rows, count * rank)
    def up(low_m, m):
        got = None
        for h in range(2):
            lhs = low_m.reshape(rows, count, rank // 2, 2)[..., h].reshape(rows, count * rank // 2)
            rhs = sel_out[:, m, :, h * heads_width:(h + 1) * heads_width].reshape(count * rank // 2, heads_width)
            term = jnp.dot(lhs, rhs, preferred_element_type=jnp.float32)
            got = term if got is None else got + term
        return got

    delta_q = up(low_q, 0)
    delta_v = up(low_v, 1)
    delta_q = lax.reduce_precision(adapter_scale * delta_q, exponent_bits=8, mantissa_bits=7)
    delta_v = lax.reduce_precision(adapter_scale * delta_v, exponent_bits=8, mantissa_bits=7)

    base = jnp.einsum("td,jde->jte", normed, qkv_weight, preferred_element_type=jnp.float32)
    query = (base[0] + delta_q).astype(jnp.bfloat16)
    keys = base[1].astype(jnp.bfloat16)
    value = (base[2] + delta_v).astype(jnp.bfloat16)
    return attend_kernel(query, keys, value, request_entry, heads_width // HEAD, HEAD, count)


def torus_mesh(mesh):
    devs = mesh.devices
    n_req, n_tp = devs.shape
    col = devs[:, 0]
    try:
        n_y = len({d.coords[1] for d in col})
        n_z = len({d.coords[2] for d in col})
        n_c = len({d.core_on_chip for d in col})
    except AttributeError:
        n_y, n_z, n_c = n_req, 1, 1
    if n_y * n_z * n_c != n_req:
        n_y, n_z, n_c = n_req, 1, 1
    return Mesh(np.asarray(devs).reshape(n_y, n_z, n_c, n_tp), ("ry", "rz", "rc", "tp"))


def solution(mesh):
    grid = torus_mesh(mesh)
    req = ("ry", "rz", "rc")
    in_specs = (
        P(req, "tp"),
        P(),
        P(None, None, "tp"),
        P(req, "tp", None),
        P(req, None, None, "tp"),
        P(req, None),
        P(req, None),
        P(req, None),
    )
    out_specs = P(req, "tp")
    return jax.shard_map(shards, mesh=grid, in_specs=in_specs, out_specs=out_specs, check_vma=False)
```

```python
import jax
import jax.numpy as jnp
import numpy as np
from jax import lax
from jax.experimental import pallas as pl
from jax.sharding import Mesh, PartitionSpec as P

HEAD = 64
LMAX = 16
LANES = 128


adapter_scale = 2.0
norm_eps = 1e-06


def attend(query, keys, value, request_entry, heads, head):
    rows = query.shape[0]
    block = min(512, rows)
    margin = LMAX
    pad_k = jnp.pad(keys, ((margin, margin), (0, 0)))
    pad_v = jnp.pad(value, ((margin, margin), (0, 0)))
    pad_r = jnp.pad(request_entry, (margin, margin), constant_values=-1)
    span = block + 2 * margin
    q_blk = query.reshape(block, heads, head)
    k_blk = pad_k.reshape(span, heads, head)
    v_blk = pad_v.reshape(span, heads, head)
    same = request_entry[:, None] == pad_r[None, :]
    scores = jnp.einsum(
        "qhd,khd->hqk", q_blk, k_blk, preferred_element_type=jnp.float32
    ) * head ** (-0.5)
    scores = jnp.where(same[None], scores, -jnp.inf)
    top = jnp.max(scores, axis=2, keepdims=True)
    expo = jnp.exp(scores - top)
    weights = (expo / jnp.sum(expo, axis=2, keepdims=True)).astype(jnp.bfloat16)
    mixed = jnp.einsum("hqk,khd->qhd", weights, v_blk, preferred_element_type=jnp.float32)
    outputs = mixed.reshape(block, heads * head)
    return outputs


def attend_kernel(query, keys, value, request_entry, heads, head, count, interpret=False):
    rows, cols = query.shape

    def body(q_ref, k_ref, v_ref, rc_ref, rr_ref, o_ref):
        same = rc_ref[...] == rr_ref[...]
        live = rc_ref[...] < count
        for h in range(heads):
            sl = slice(h * head, (h + 1) * head)
            scores = lax.dot_general(
                q_ref[:, sl], k_ref[:, sl], (((1,), (1,)), ((), ())),
                preferred_element_type=jnp.float32,
            ) * head ** (-0.5)
            scores = jnp.where(same, scores, -jnp.inf)
            top = jnp.max(scores, axis=1, keepdims=True)
            expo = jnp.exp(scores - top)
            weights = (expo / jnp.sum(expo, axis=1, keepdims=True)).astype(jnp.bfloat16)
            mixed = jnp.dot(weights, v_ref[:, sl], preferred_element_type=jnp.float32)
            o_ref[:, sl] = jnp.where(live, mixed, 0.0).astype(jnp.bfloat16)

    return pl.pallas_call(
        body,
        out_shape=jax.ShapeDtypeStruct((rows, cols), jnp.bfloat16),
        interpret=interpret,
    )(query, keys, value, request_entry.reshape(rows, 1), request_entry.reshape(1, rows))


def exchange(value, axis, pairs):
    return lax.ppermute(value, axis, pairs)


def ring_gather(value, axis, n):
    rel = [None] * n
    rel[0] = value
    cw = value
    ccw = value
    for s in range(1, n // 2 + 1):
        cw = exchange(cw, axis, [(i, (i + 1) % n) for i in range(n)])
        rel[(n - s) % n] = cw
        if s < n - s:
            ccw = exchange(ccw, axis, [(i, (i - 1) % n) for i in range(n)])
            rel[s] = ccw
    return jnp.stack(rel)


def doubling_sources(n):
    return n > 1 and (n & (n - 1)) == 0


def shards(tokens, gain, qkv_weight, adapter_in, adapter_out, request_of, adapter_of, block_row):
    width = tokens.shape[1]
    rank2 = adapter_in.shape[2]
    rank = rank2 // 2
    heads_width = qkv_weight.shape[2]
    n_tp = lax.axis_size("tp")
    n_y, n_z, n_c = lax.axis_size("ry"), lax.axis_size("rz"), lax.axis_size("rc")
    split = lax.axis_index("tp")
    my_y, my_z, my_c = lax.axis_index("ry"), lax.axis_index("rz"), lax.axis_index("rc")

    request_entry = request_of[0]
    adapters = adapter_of[0]
    count = adapters.shape[0]
    rows = request_entry.shape[0]
    onehot = request_entry[:, None] == jnp.arange(count, dtype=jnp.int32)[None, :]
    live = request_entry < count

    if doubling_sources(n_tp):
        pieces, sources = [tokens], [split]
        k = 1
        while k < n_tp:
            got = exchange(jnp.stack(pieces), "tp", [(i, i ^ k) for i in range(n_tp)])
            pieces = pieces + [got[j] for j in range(got.shape[0])]
            sources = sources + [src ^ k for src in sources]
            k *= 2
    else:
        pieces, sources = [tokens], [split]
        for s in range(1, n_tp):
            pieces.append(exchange(tokens, "tp", [(i, (i + s) % n_tp) for i in range(n_tp)]))
            sources.append((split - s) % n_tp)

    n_in = adapter_in.shape[1]
    lane_w = 2 * heads_width
    down_t = adapter_in[0].T
    up_rows = adapter_out[0].reshape(2 * rank // 2, lane_w)
    packed = jnp.concatenate([down_t, up_rows], axis=0)
    per = packed.shape[0]
    if n_c > 1:
        partner = exchange(adapters, "rc", [(i, (i + 1) % n_c) for i in range(n_c)])
    every = lax.all_to_all(
        jnp.broadcast_to(packed[None], (n_z,) + packed.shape).reshape(n_z * per, lane_w),
        "rz", split_axis=0, concat_axis=0, tiled=True,
    )
    every = lax.all_gather(every, "ry", axis=0, tiled=True).reshape(n_y * n_z, per, lane_w)

    def place(ads):
        a_c = ads % n_c
        a_z = (ads // n_c) % n_z
        a_y = ads // (n_c * n_z)
        return a_y * n_z + a_z, a_c

    n_held = n_y * n_z
    table = every.reshape(n_held, per * lane_w)

    def pick(places):
        hot = (places[:, None] == jnp.arange(n_held, dtype=jnp.int32)[None, :]).astype(jnp.bfloat16)
        got = jnp.dot(hot, table, preferred_element_type=jnp.float32)
        return got.astype(jnp.bfloat16).reshape(places.shape[0], per, lane_w)

    here, a_c = place(adapters)
    if n_c > 1:
        there, _ = place(partner)
        for_partner = jnp.take(every, there, axis=0)
        every, for_partner = lax.optimization_barrier((every, for_partner))
        table = every.reshape(n_held, per * lane_w)
        sent = exchange(for_partner, "rc", [(i, (i - 1) % n_c) for i in range(n_c)])
        sel = pick(here)
        sel = jnp.where((a_c == my_c)[:, None, None], sel, sent)
    else:
        sel = pick(here)
    sel_in = sel[:, :rank2]
    sel_out = sel[:, rank2:].reshape(count, 2, rank // 2, lane_w)

    wide = [p.astype(jnp.float32) for p in pieces]
    power = sum(jnp.sum(w * w, axis=1, keepdims=True) for w in wide) / (width * n_tp)
    scale = lax.rsqrt(power + norm_eps)
    normed = jnp.zeros((rows, width * n_tp), jnp.bfloat16)
    own = None
    for s, (w, src) in enumerate(zip(wide, sources)):
        g = lax.dynamic_slice_in_dim(gain, src * width, width)
        piece = (w * scale * g).astype(jnp.bfloat16)
        if s == 0:
            own = piece
        normed = lax.dynamic_update_slice_in_dim(normed, piece, src * width, 1)

    part = jnp.einsum("td,rkd->trk", own, sel_in, preferred_element_type=jnp.float32)
    part = jnp.sum(jnp.where(onehot[:, :, None], part, 0.0), axis=1)
    if doubling_sources(n_tp):
        total = part
        k = 1
        while k < n_tp:
            total = total + exchange(total, "tp", [(i, i ^ k) for i in range(n_tp)])
            k *= 2
    else:
        total = part
        for s in range(1, n_tp):
            total = total + exchange(part, "tp", [(i, (i + s) % n_tp) for i in range(n_tp)])
    low = total.astype(jnp.bfloat16)

    zero = jnp.zeros((), jnp.bfloat16)
    low_q = jnp.where(onehot[:, :, None], low[:, None, :rank], zero).reshape(rows, count * rank)
    low_v = jnp.where(onehot[:, :, None], low[:, None, rank:], zero).reshape(rows, count * rank)
    def up(low_m, m):
        got = None
        for h in range(2):
            lhs = low_m.reshape(rows, count, rank // 2, 2)[..., h].reshape(rows, count * rank // 2)
            rhs = sel_out[:, m, :, h * heads_width:(h + 1) * heads_width].reshape(count * rank // 2, heads_width)
            term = jnp.dot(lhs, rhs, preferred_element_type=jnp.float32)
            got = term if got is None else got + term
        return got

    delta_q = up(low_q, 0)
    delta_v = up(low_v, 1)
    delta_q = lax.reduce_precision(adapter_scale * delta_q, exponent_bits=8, mantissa_bits=7)
    delta_v = lax.reduce_precision(adapter_scale * delta_v, exponent_bits=8, mantissa_bits=7)

    base = jnp.einsum("td,jde->jte", normed, qkv_weight, preferred_element_type=jnp.float32)
    query = (base[0] + delta_q).astype(jnp.bfloat16)
    keys = base[1].astype(jnp.bfloat16)
    value = (base[2] + delta_v).astype(jnp.bfloat16)
    return attend_kernel(query, keys, value, request_entry, heads_width // HEAD, HEAD, count)


def torus_mesh(mesh):
    devs = mesh.devices
    n_req, n_tp = devs.shape
    col = devs[:, 0]
    try:
        n_y = len({d.coords[1] for d in col})
        n_z = len({d.coords[2] for d in col})
        n_c = len({d.core_on_chip for d in col})
    except AttributeError:
        n_y, n_z, n_c = n_req, 1, 1
    if n_y * n_z * n_c != n_req:
        n_y, n_z, n_c = n_req, 1, 1
    return Mesh(np.asarray(devs).reshape(n_y, n_z, n_c, n_tp), ("ry", "rz", "rc", "tp"))


def solution(mesh):
    grid = torus_mesh(mesh)
    req = ("ry", "rz", "rc")
    in_specs = (
        P(req, "tp"),
        P(),
        P(None, None, "tp"),
        P(req, "tp", None),
        P(req, None, None, "tp"),
        P(req, None),
        P(req, None),
        P(req, None),
    )
    out_specs = P(req, "tp")
    return jax.shard_map(shards, mesh=grid, in_specs=in_specs, out_specs=out_specs, check_vma=False)
```

```python
import jax
import jax.numpy as jnp
import numpy as np
from jax import lax
from jax.experimental import pallas as pl
from jax.sharding import Mesh, PartitionSpec as P

HEAD = 64
LMAX = 16
LANES = 128


adapter_scale = 2.0
norm_eps = 1e-06


def attend(query, keys, value, request_entry, heads, head):
    rows = query.shape[0]
    block = min(512, rows)
    margin = LMAX
    pad_k = jnp.pad(keys, ((margin, margin), (0, 0)))
    pad_v = jnp.pad(value, ((margin, margin), (0, 0)))
    pad_r = jnp.pad(request_entry, (margin, margin), constant_values=-1)
    span = block + 2 * margin
    q_blk = query.reshape(block, heads, head)
    k_blk = pad_k.reshape(span, heads, head)
    v_blk = pad_v.reshape(span, heads, head)
    same = request_entry[:, None] == pad_r[None, :]
    scores = jnp.einsum(
        "qhd,khd->hqk", q_blk, k_blk, preferred_element_type=jnp.float32
    ) * head ** (-0.5)
    scores = jnp.where(same[None], scores, -jnp.inf)
    top = jnp.max(scores, axis=2, keepdims=True)
    expo = jnp.exp(scores - top)
    weights = (expo / jnp.sum(expo, axis=2, keepdims=True)).astype(jnp.bfloat16)
    mixed = jnp.einsum("hqk,khd->qhd", weights, v_blk, preferred_element_type=jnp.float32)
    outputs = mixed.reshape(block, heads * head)
    return outputs


def attend_kernel(query, keys, value, request_entry, heads, head, count, interpret=False):
    rows, cols = query.shape

    def body(q_ref, k_ref, v_ref, rc_ref, rr_ref, o_ref):
        same = rc_ref[...] == rr_ref[...]
        live = rc_ref[...] < count
        for h in range(heads):
            sl = slice(h * head, (h + 1) * head)
            scores = lax.dot_general(
                q_ref[:, sl], k_ref[:, sl], (((1,), (1,)), ((), ())),
                preferred_element_type=jnp.float32,
            ) * head ** (-0.5)
            scores = jnp.where(same, scores, -jnp.inf)
            top = jnp.max(scores, axis=1, keepdims=True)
            expo = jnp.exp(scores - top)
            weights = (expo / jnp.sum(expo, axis=1, keepdims=True)).astype(jnp.bfloat16)
            mixed = jnp.dot(weights, v_ref[:, sl], preferred_element_type=jnp.float32)
            o_ref[:, sl] = jnp.where(live, mixed, 0.0).astype(jnp.bfloat16)

    return pl.pallas_call(
        body,
        out_shape=jax.ShapeDtypeStruct((rows, cols), jnp.bfloat16),
        interpret=interpret,
    )(query, keys, value, request_entry.reshape(rows, 1), request_entry.reshape(1, rows))


def exchange(value, axis, pairs):
    return lax.ppermute(value, axis, pairs)


def ring_gather(value, axis, n):
    rel = [None] * n
    rel[0] = value
    cw = value
    ccw = value
    for s in range(1, n // 2 + 1):
        cw = exchange(cw, axis, [(i, (i + 1) % n) for i in range(n)])
        rel[(n - s) % n] = cw
        if s < n - s:
            ccw = exchange(ccw, axis, [(i, (i - 1) % n) for i in range(n)])
            rel[s] = ccw
    return jnp.stack(rel)


def doubling_sources(n):
    return n > 1 and (n & (n - 1)) == 0


def shards(tokens, gain, qkv_weight, adapter_in, adapter_out, request_of, adapter_of, block_row):
    width = tokens.shape[1]
    rank2 = adapter_in.shape[2]
    rank = rank2 // 2
    heads_width = qkv_weight.shape[2]
    n_tp = lax.axis_size("tp")
    n_y, n_z, n_c = lax.axis_size("ry"), lax.axis_size("rz"), lax.axis_size("rc")
    split = lax.axis_index("tp")
    my_y, my_z, my_c = lax.axis_index("ry"), lax.axis_index("rz"), lax.axis_index("rc")

    request_entry = request_of[0]
    adapters = adapter_of[0]
    count = adapters.shape[0]
    rows = request_entry.shape[0]
    onehot = request_entry[:, None] == jnp.arange(count, dtype=jnp.int32)[None, :]
    live = request_entry < count

    if doubling_sources(n_tp):
        pieces, sources = [tokens], [split]
        k = 1
        while k < n_tp:
            got = exchange(jnp.stack(pieces), "tp", [(i, i ^ k) for i in range(n_tp)])
            pieces = pieces + [got[j] for j in range(got.shape[0])]
            sources = sources + [src ^ k for src in sources]
            k *= 2
    else:
        pieces, sources = [tokens], [split]
        for s in range(1, n_tp):
            pieces.append(exchange(tokens, "tp", [(i, (i + s) % n_tp) for i in range(n_tp)]))
            sources.append((split - s) % n_tp)

    n_in = adapter_in.shape[1]
    lane_w = 2 * heads_width
    down_t = adapter_in[0].T
    up_rows = adapter_out[0].reshape(2 * rank // 2, lane_w)
    packed = jnp.concatenate([down_t, up_rows], axis=0)
    per = packed.shape[0]
    if n_c > 1:
        partner = exchange(adapters, "rc", [(i, (i + 1) % n_c) for i in range(n_c)])
    every = lax.all_to_all(
        jnp.broadcast_to(packed[None], (n_z,) + packed.shape).reshape(n_z * per, lane_w),
        "rz", split_axis=0, concat_axis=0, tiled=True,
    )
    every = lax.all_gather(every, "ry", axis=0, tiled=True).reshape(n_y * n_z, per, lane_w)

    def place(ads):
        a_c = ads % n_c
        a_z = (ads // n_c) % n_z
        a_y = ads // (n_c * n_z)
        return a_y * n_z + a_z, a_c

    n_held = n_y * n_z
    table = every.reshape(n_held, per * lane_w)

    def pick(places):
        hot = (places[:, None] == jnp.arange(n_held, dtype=jnp.int32)[None, :]).astype(jnp.bfloat16)
        got = jnp.dot(hot, table, preferred_element_type=jnp.float32)
        return got.astype(jnp.bfloat16).reshape(places.shape[0], per, lane_w)

    here, a_c = place(adapters)
    if n_c > 1:
        there, _ = place(partner)
        for_partner = jnp.take(every, there, axis=0)
        every, for_partner = lax.optimization_barrier((every, for_partner))
        table = every.reshape(n_held, per * lane_w)
        sent = exchange(for_partner, "rc", [(i, (i - 1) % n_c) for i in range(n_c)])
        sel = pick(here)
        sel = jnp.where((a_c == my_c)[:, None, None], sel, sent)
    else:
        sel = pick(here)
    sel_in = sel[:, :rank2]
    sel_out = sel[:, rank2:].reshape(count, 2, rank // 2, lane_w)

    wide = [p.astype(jnp.float32) for p in pieces]
    power = sum(jnp.sum(w * w, axis=1, keepdims=True) for w in wide) / (width * n_tp)
    scale = lax.rsqrt(power + norm_eps)
    normed = jnp.zeros((rows, width * n_tp), jnp.bfloat16)
    own = None
    for s, (w, src) in enumerate(zip(wide, sources)):
        g = lax.dynamic_slice_in_dim(gain, src * width, width)
        piece = (w * scale * g).astype(jnp.bfloat16)
        if s == 0:
            own = piece
        normed = lax.dynamic_update_slice_in_dim(normed, piece, src * width, 1)

    part = jnp.einsum("td,rkd->trk", own, sel_in, preferred_element_type=jnp.float32)
    part = jnp.sum(jnp.where(onehot[:, :, None], part, 0.0), axis=1)
    partials = lax.all_to_all(
        jnp.broadcast_to(part[None], (n_tp,) + part.shape), "tp", split_axis=0, concat_axis=0, tiled=True
    )
    total = partials[0]
    for s in range(1, n_tp):
        total = total + partials[s]
    low = total.astype(jnp.bfloat16)

    zero = jnp.zeros((), jnp.bfloat16)
    low_q = jnp.where(onehot[:, :, None], low[:, None, :rank], zero).reshape(rows, count * rank)
    low_v = jnp.where(onehot[:, :, None], low[:, None, rank:], zero).reshape(rows, count * rank)
    def up(low_m, m):
        got = None
        for h in range(2):
            lhs = low_m.reshape(rows, count, rank // 2, 2)[..., h].reshape(rows, count * rank // 2)
            rhs = sel_out[:, m, :, h * heads_width:(h + 1) * heads_width].reshape(count * rank // 2, heads_width)
            term = jnp.dot(lhs, rhs, preferred_element_type=jnp.float32)
            got = term if got is None else got + term
        return got

    delta_q = up(low_q, 0)
    delta_v = up(low_v, 1)
    delta_q = lax.reduce_precision(adapter_scale * delta_q, exponent_bits=8, mantissa_bits=7)
    delta_v = lax.reduce_precision(adapter_scale * delta_v, exponent_bits=8, mantissa_bits=7)

    base = jnp.einsum("td,jde->jte", normed, qkv_weight, preferred_element_type=jnp.float32)
    query = (base[0] + delta_q).astype(jnp.bfloat16)
    keys = base[1].astype(jnp.bfloat16)
    value = (base[2] + delta_v).astype(jnp.bfloat16)
    return attend_kernel(query, keys, value, request_entry, heads_width // HEAD, HEAD, count)


def torus_mesh(mesh):
    devs = mesh.devices
    n_req, n_tp = devs.shape
    col = devs[:, 0]
    try:
        n_y = len({d.coords[1] for d in col})
        n_z = len({d.coords[2] for d in col})
        n_c = len({d.core_on_chip for d in col})
    except AttributeError:
        n_y, n_z, n_c = n_req, 1, 1
    if n_y * n_z * n_c != n_req:
        n_y, n_z, n_c = n_req, 1, 1
    return Mesh(np.asarray(devs).reshape(n_y, n_z, n_c, n_tp), ("ry", "rz", "rc", "tp"))


def solution(mesh):
    grid = torus_mesh(mesh)
    req = ("ry", "rz", "rc")
    in_specs = (
        P(req, "tp"),
        P(),
        P(None, None, "tp"),
        P(req, "tp", None),
        P(req, None, None, "tp"),
        P(req, None),
        P(req, None),
        P(req, None),
    )
    out_specs = P(req, "tp")
    return jax.shard_map(shards, mesh=grid, in_specs=in_specs, out_specs=out_specs, check_vma=False)
```

```python
import jax
import jax.numpy as jnp
import numpy as np
from jax import lax
from jax.experimental import pallas as pl
from jax.sharding import Mesh, PartitionSpec as P

HEAD = 64
LMAX = 16
LANES = 128


adapter_scale = 2.0
norm_eps = 1e-06


def attend(query, keys, value, request_entry, heads, head):
    rows = query.shape[0]
    block = min(512, rows)
    margin = LMAX
    pad_k = jnp.pad(keys, ((margin, margin), (0, 0)))
    pad_v = jnp.pad(value, ((margin, margin), (0, 0)))
    pad_r = jnp.pad(request_entry, (margin, margin), constant_values=-1)
    span = block + 2 * margin
    q_blk = query.reshape(block, heads, head)
    k_blk = pad_k.reshape(span, heads, head)
    v_blk = pad_v.reshape(span, heads, head)
    same = request_entry[:, None] == pad_r[None, :]
    scores = jnp.einsum(
        "qhd,khd->hqk", q_blk, k_blk, preferred_element_type=jnp.float32
    ) * head ** (-0.5)
    scores = jnp.where(same[None], scores, -jnp.inf)
    top = jnp.max(scores, axis=2, keepdims=True)
    expo = jnp.exp(scores - top)
    weights = (expo / jnp.sum(expo, axis=2, keepdims=True)).astype(jnp.bfloat16)
    mixed = jnp.einsum("hqk,khd->qhd", weights, v_blk, preferred_element_type=jnp.float32)
    outputs = mixed.reshape(block, heads * head)
    return outputs


def attend_kernel(query, keys, value, request_entry, heads, head, count, interpret=False):
    rows, cols = query.shape

    def body(q_ref, k_ref, v_ref, rc_ref, rr_ref, o_ref):
        same = rc_ref[...] == rr_ref[...]
        live = rc_ref[...] < count
        for h in range(heads):
            sl = slice(h * head, (h + 1) * head)
            scores = lax.dot_general(
                q_ref[:, sl], k_ref[:, sl], (((1,), (1,)), ((), ())),
                preferred_element_type=jnp.float32,
            ) * head ** (-0.5)
            scores = jnp.where(same, scores, -jnp.inf)
            top = jnp.max(scores, axis=1, keepdims=True)
            expo = jnp.exp(scores - top)
            weights = (expo / jnp.sum(expo, axis=1, keepdims=True)).astype(jnp.bfloat16)
            mixed = jnp.dot(weights, v_ref[:, sl], preferred_element_type=jnp.float32)
            o_ref[:, sl] = jnp.where(live, mixed, 0.0).astype(jnp.bfloat16)

    return pl.pallas_call(
        body,
        out_shape=jax.ShapeDtypeStruct((rows, cols), jnp.bfloat16),
        interpret=interpret,
    )(query, keys, value, request_entry.reshape(rows, 1), request_entry.reshape(1, rows))


def exchange(value, axis, pairs):
    return lax.ppermute(value, axis, pairs)


def ring_gather(value, axis, n):
    rel = [None] * n
    rel[0] = value
    cw = value
    ccw = value
    for s in range(1, n // 2 + 1):
        cw = exchange(cw, axis, [(i, (i + 1) % n) for i in range(n)])
        rel[(n - s) % n] = cw
        if s < n - s:
            ccw = exchange(ccw, axis, [(i, (i - 1) % n) for i in range(n)])
            rel[s] = ccw
    return jnp.stack(rel)


def doubling_sources(n):
    return n > 1 and (n & (n - 1)) == 0


def shards(tokens, gain, qkv_weight, adapter_in, adapter_out, request_of, adapter_of, block_row):
    width = tokens.shape[1]
    rank2 = adapter_in.shape[2]
    rank = rank2 // 2
    heads_width = qkv_weight.shape[2]
    n_tp = lax.axis_size("tp")
    n_y, n_z, n_c = lax.axis_size("ry"), lax.axis_size("rz"), lax.axis_size("rc")
    split = lax.axis_index("tp")
    my_y, my_z, my_c = lax.axis_index("ry"), lax.axis_index("rz"), lax.axis_index("rc")

    request_entry = request_of[0]
    adapters = adapter_of[0]
    count = adapters.shape[0]
    rows = request_entry.shape[0]
    onehot = request_entry[:, None] == jnp.arange(count, dtype=jnp.int32)[None, :]
    live = request_entry < count

    if doubling_sources(n_tp):
        pieces, sources = [tokens], [split]
        k = 1
        while k < n_tp:
            got = exchange(jnp.stack(pieces), "tp", [(i, i ^ k) for i in range(n_tp)])
            pieces = pieces + [got[j] for j in range(got.shape[0])]
            sources = sources + [src ^ k for src in sources]
            k *= 2
    else:
        pieces, sources = [tokens], [split]
        for s in range(1, n_tp):
            pieces.append(exchange(tokens, "tp", [(i, (i + s) % n_tp) for i in range(n_tp)]))
            sources.append((split - s) % n_tp)

    n_in = adapter_in.shape[1]
    lane_w = 2 * heads_width
    down_t = adapter_in[0].T
    up_rows = adapter_out[0].reshape(2 * rank // 2, lane_w)
    packed = jnp.concatenate([down_t, up_rows], axis=0)
    per = packed.shape[0]
    if n_c > 1:
        partner = exchange(adapters, "rc", [(i, (i + 1) % n_c) for i in range(n_c)])
    every = lax.all_to_all(
        jnp.broadcast_to(packed[None], (n_z,) + packed.shape).reshape(n_z * per, lane_w),
        "rz", split_axis=0, concat_axis=0, tiled=True,
    )
    every = lax.all_gather(every, "ry", axis=0, tiled=True).reshape(n_y * n_z, per, lane_w)

    wide = [p.astype(jnp.float32) for p in pieces]
    power = sum(jnp.sum(w * w, axis=1, keepdims=True) for w in wide) / (width * n_tp)
    scale = lax.rsqrt(power + norm_eps)
    normed = jnp.zeros((rows, width * n_tp), jnp.bfloat16)
    own = None
    for s, (w, src) in enumerate(zip(wide, sources)):
        g = lax.dynamic_slice_in_dim(gain, src * width, width)
        piece = (w * scale * g).astype(jnp.bfloat16)
        if s == 0:
            own = piece
        normed = lax.dynamic_update_slice_in_dim(normed, piece, src * width, 1)

    base = jnp.einsum("td,jde->jte", normed, qkv_weight, preferred_element_type=jnp.float32)

    def place(ads):
        a_c = ads % n_c
        a_z = (ads // n_c) % n_z
        a_y = ads // (n_c * n_z)
        return a_y * n_z + a_z, a_c

    n_held = n_y * n_z
    table = every.reshape(n_held, per * lane_w)

    def pick(places):
        hot = (places[:, None] == jnp.arange(n_held, dtype=jnp.int32)[None, :]).astype(jnp.bfloat16)
        got = jnp.dot(hot, table, preferred_element_type=jnp.float32)
        return got.astype(jnp.bfloat16).reshape(places.shape[0], per, lane_w)

    here, a_c = place(adapters)
    if n_c > 1:
        partner, base = lax.optimization_barrier((partner, base))
        there, _ = place(partner)
        for_partner = jnp.take(every, there, axis=0, mode="clip")
        every, for_partner = lax.optimization_barrier((every, for_partner))
        table = every.reshape(n_held, per * lane_w)
        sent = exchange(for_partner, "rc", [(i, (i - 1) % n_c) for i in range(n_c)])
        sel = pick(here)
        sel = jnp.where((a_c == my_c)[:, None, None], sel, sent)
    else:
        sel = pick(here)
    sel_in = sel[:, :rank2]
    sel_out = sel[:, rank2:].reshape(count, 2, rank // 2, lane_w)

    part = jnp.einsum("td,rkd->trk", own, sel_in, preferred_element_type=jnp.float32)
    part = jnp.sum(jnp.where(onehot[:, :, None], part, 0.0), axis=1)
    partials = lax.all_to_all(
        jnp.broadcast_to(part[None], (n_tp,) + part.shape), "tp", split_axis=0, concat_axis=0, tiled=True
    )
    total = partials[0]
    for s in range(1, n_tp):
        total = total + partials[s]
    low = total.astype(jnp.bfloat16)

    zero = jnp.zeros((), jnp.bfloat16)
    low_q = jnp.where(onehot[:, :, None], low[:, None, :rank], zero).reshape(rows, count * rank)
    low_v = jnp.where(onehot[:, :, None], low[:, None, rank:], zero).reshape(rows, count * rank)
    def up(low_m, m):
        got = None
        for h in range(2):
            lhs = low_m.reshape(rows, count, rank // 2, 2)[..., h].reshape(rows, count * rank // 2)
            rhs = sel_out[:, m, :, h * heads_width:(h + 1) * heads_width].reshape(count * rank // 2, heads_width)
            term = jnp.dot(lhs, rhs, preferred_element_type=jnp.float32)
            got = term if got is None else got + term
        return got

    delta_q = up(low_q, 0)
    delta_v = up(low_v, 1)
    delta_q = lax.reduce_precision(adapter_scale * delta_q, exponent_bits=8, mantissa_bits=7)
    delta_v = lax.reduce_precision(adapter_scale * delta_v, exponent_bits=8, mantissa_bits=7)

    query = (base[0] + delta_q).astype(jnp.bfloat16)
    keys = base[1].astype(jnp.bfloat16)
    value = (base[2] + delta_v).astype(jnp.bfloat16)
    return attend_kernel(query, keys, value, request_entry, heads_width // HEAD, HEAD, count)


def torus_mesh(mesh):
    devs = mesh.devices
    n_req, n_tp = devs.shape
    col = devs[:, 0]
    try:
        n_y = len({d.coords[1] for d in col})
        n_z = len({d.coords[2] for d in col})
        n_c = len({d.core_on_chip for d in col})
    except AttributeError:
        n_y, n_z, n_c = n_req, 1, 1
    if n_y * n_z * n_c != n_req:
        n_y, n_z, n_c = n_req, 1, 1
    return Mesh(np.asarray(devs).reshape(n_y, n_z, n_c, n_tp), ("ry", "rz", "rc", "tp"))


def solution(mesh):
    grid = torus_mesh(mesh)
    req = ("ry", "rz", "rc")
    in_specs = (
        P(req, "tp"),
        P(),
        P(None, None, "tp"),
        P(req, "tp", None),
        P(req, None, None, "tp"),
        P(req, None),
        P(req, None),
        P(req, None),
    )
    out_specs = P(req, "tp")
    return jax.shard_map(shards, mesh=grid, in_specs=in_specs, out_specs=out_specs, check_vma=False)
```

```python
import jax
import jax.numpy as jnp
import numpy as np
from jax import lax
from jax.experimental import pallas as pl
from jax.sharding import Mesh, PartitionSpec as P

HEAD = 64
LMAX = 16
LANES = 128


adapter_scale = 2.0
norm_eps = 1e-06


def attend(query, keys, value, request_entry, heads, head):
    rows = query.shape[0]
    block = min(512, rows)
    margin = LMAX
    pad_k = jnp.pad(keys, ((margin, margin), (0, 0)))
    pad_v = jnp.pad(value, ((margin, margin), (0, 0)))
    pad_r = jnp.pad(request_entry, (margin, margin), constant_values=-1)
    span = block + 2 * margin
    q_blk = query.reshape(block, heads, head)
    k_blk = pad_k.reshape(span, heads, head)
    v_blk = pad_v.reshape(span, heads, head)
    same = request_entry[:, None] == pad_r[None, :]
    scores = jnp.einsum(
        "qhd,khd->hqk", q_blk, k_blk, preferred_element_type=jnp.float32
    ) * head ** (-0.5)
    scores = jnp.where(same[None], scores, -jnp.inf)
    top = jnp.max(scores, axis=2, keepdims=True)
    expo = jnp.exp(scores - top)
    weights = (expo / jnp.sum(expo, axis=2, keepdims=True)).astype(jnp.bfloat16)
    mixed = jnp.einsum("hqk,khd->qhd", weights, v_blk, preferred_element_type=jnp.float32)
    outputs = mixed.reshape(block, heads * head)
    return outputs


def attend_kernel(query, keys, value, request_entry, heads, head, count, interpret=False):
    rows, cols = query.shape

    def body(q_ref, k_ref, v_ref, rc_ref, rr_ref, o_ref):
        same = rc_ref[...] == rr_ref[...]
        live = rc_ref[...] < count
        for h in range(heads):
            sl = slice(h * head, (h + 1) * head)
            scores = lax.dot_general(
                q_ref[:, sl], k_ref[:, sl], (((1,), (1,)), ((), ())),
                preferred_element_type=jnp.float32,
            ) * head ** (-0.5)
            scores = jnp.where(same, scores, -jnp.inf)
            top = jnp.max(scores, axis=1, keepdims=True)
            expo = jnp.exp(scores - top)
            weights = (expo / jnp.sum(expo, axis=1, keepdims=True)).astype(jnp.bfloat16)
            mixed = jnp.dot(weights, v_ref[:, sl], preferred_element_type=jnp.float32)
            o_ref[:, sl] = jnp.where(live, mixed, 0.0).astype(jnp.bfloat16)

    return pl.pallas_call(
        body,
        out_shape=jax.ShapeDtypeStruct((rows, cols), jnp.bfloat16),
        interpret=interpret,
    )(query, keys, value, request_entry.reshape(rows, 1), request_entry.reshape(1, rows))


def exchange(value, axis, pairs):
    return lax.ppermute(value, axis, pairs)


def ring_gather(value, axis, n):
    rel = [None] * n
    rel[0] = value
    cw = value
    ccw = value
    for s in range(1, n // 2 + 1):
        cw = exchange(cw, axis, [(i, (i + 1) % n) for i in range(n)])
        rel[(n - s) % n] = cw
        if s < n - s:
            ccw = exchange(ccw, axis, [(i, (i - 1) % n) for i in range(n)])
            rel[s] = ccw
    return jnp.stack(rel)


def doubling_sources(n):
    return n > 1 and (n & (n - 1)) == 0


def shards(tokens, gain, qkv_weight, adapter_in, adapter_out, request_of, adapter_of, block_row):
    width = tokens.shape[1]
    rank2 = adapter_in.shape[2]
    rank = rank2 // 2
    heads_width = qkv_weight.shape[2]
    n_tp = lax.axis_size("tp")
    n_y, n_z, n_c = lax.axis_size("ry"), lax.axis_size("rz"), lax.axis_size("rc")
    split = lax.axis_index("tp")
    my_y, my_z, my_c = lax.axis_index("ry"), lax.axis_index("rz"), lax.axis_index("rc")

    request_entry = request_of[0]
    adapters = adapter_of[0]
    count = adapters.shape[0]
    rows = request_entry.shape[0]
    onehot = request_entry[:, None] == jnp.arange(count, dtype=jnp.int32)[None, :]
    live = request_entry < count

    if doubling_sources(n_tp):
        pieces, sources = [tokens], [split]
        k = 1
        while k < n_tp:
            got = exchange(jnp.stack(pieces), "tp", [(i, i ^ k) for i in range(n_tp)])
            pieces = pieces + [got[j] for j in range(got.shape[0])]
            sources = sources + [src ^ k for src in sources]
            k *= 2
    else:
        pieces, sources = [tokens], [split]
        for s in range(1, n_tp):
            pieces.append(exchange(tokens, "tp", [(i, (i + s) % n_tp) for i in range(n_tp)]))
            sources.append((split - s) % n_tp)

    n_in = adapter_in.shape[1]
    lane_w = 2 * heads_width
    down_t = adapter_in[0].T
    up_rows = adapter_out[0].reshape(2 * rank // 2, lane_w)
    packed = jnp.concatenate([down_t, up_rows], axis=0)
    per = packed.shape[0]
    if n_c > 1:
        partner = exchange(adapters, "rc", [(i, (i + 1) % n_c) for i in range(n_c)])
    every = lax.all_to_all(
        jnp.broadcast_to(packed[None], (n_z,) + packed.shape).reshape(n_z * per, lane_w),
        "rz", split_axis=0, concat_axis=0, tiled=True,
    )
    every = lax.all_gather(every, "ry", axis=0, tiled=True).reshape(n_y * n_z, per, lane_w)

    def place(ads):
        a_c = ads % n_c
        a_z = (ads // n_c) % n_z
        a_y = ads // (n_c * n_z)
        return a_y * n_z + a_z, a_c

    n_held = n_y * n_z
    table = every.reshape(n_held, per * lane_w)

    def pick(places):
        hot = (places[:, None] == jnp.arange(n_held, dtype=jnp.int32)[None, :]).astype(jnp.bfloat16)
        got = jnp.dot(hot, table, preferred_element_type=jnp.float32)
        return got.astype(jnp.bfloat16).reshape(places.shape[0], per, lane_w)

    here, a_c = place(adapters)
    if n_c > 1:
        there, _ = place(partner)
        for_partner = jnp.take(every, there, axis=0, mode="clip")
        every, for_partner = lax.optimization_barrier((every, for_partner))
        table = every.reshape(n_held, per * lane_w)
        sent = exchange(for_partner, "rc", [(i, (i - 1) % n_c) for i in range(n_c)])
        sel = pick(here)
        sel = jnp.where((a_c == my_c)[:, None, None], sel, sent)
    else:
        sel = pick(here)
    sel_in = sel[:, :rank2]
    sel_out = sel[:, rank2:].reshape(count, 2, rank // 2, lane_w)

    wide = [p.astype(jnp.float32) for p in pieces]
    power = sum(jnp.sum(w * w, axis=1, keepdims=True) for w in wide) / (width * n_tp)
    scale = lax.rsqrt(power + norm_eps)
    normed = jnp.zeros((rows, width * n_tp), jnp.bfloat16)
    own = None
    for s, (w, src) in enumerate(zip(wide, sources)):
        g = lax.dynamic_slice_in_dim(gain, src * width, width)
        piece = (w * scale * g).astype(jnp.bfloat16)
        if s == 0:
            own = piece
        normed = lax.dynamic_update_slice_in_dim(normed, piece, src * width, 1)

    part = jnp.einsum("td,rkd->trk", own, sel_in, preferred_element_type=jnp.float32)
    part = jnp.sum(jnp.where(onehot[:, :, None], part, 0.0), axis=1)
    partials = lax.all_to_all(
        jnp.broadcast_to(part[None], (n_tp,) + part.shape), "tp", split_axis=0, concat_axis=0, tiled=True
    )
    total = partials[0]
    for s in range(1, n_tp):
        total = total + partials[s]
    low = total.astype(jnp.bfloat16)

    zero = jnp.zeros((), jnp.bfloat16)
    low_q = jnp.where(onehot[:, :, None], low[:, None, :rank], zero).reshape(rows, count * rank)
    low_v = jnp.where(onehot[:, :, None], low[:, None, rank:], zero).reshape(rows, count * rank)
    def up(low_m, m):
        got = None
        for h in range(2):
            lhs = low_m.reshape(rows, count, rank // 2, 2)[..., h].reshape(rows, count * rank // 2)
            rhs = sel_out[:, m, :, h * heads_width:(h + 1) * heads_width].reshape(count * rank // 2, heads_width)
            term = jnp.dot(lhs, rhs, preferred_element_type=jnp.float32)
            got = term if got is None else got + term
        return got

    delta_q = up(low_q, 0)
    delta_v = up(low_v, 1)
    delta_q = lax.reduce_precision(adapter_scale * delta_q, exponent_bits=8, mantissa_bits=7)
    delta_v = lax.reduce_precision(adapter_scale * delta_v, exponent_bits=8, mantissa_bits=7)

    base = jnp.einsum("td,jde->jte", normed, qkv_weight, preferred_element_type=jnp.float32)
    query = (base[0] + delta_q).astype(jnp.bfloat16)
    keys = base[1].astype(jnp.bfloat16)
    value = (base[2] + delta_v).astype(jnp.bfloat16)
    return attend_kernel(query, keys, value, request_entry, heads_width // HEAD, HEAD, count)


def torus_mesh(mesh):
    devs = mesh.devices
    n_req, n_tp = devs.shape
    col = devs[:, 0]
    try:
        n_y = len({d.coords[1] for d in col})
        n_z = len({d.coords[2] for d in col})
        n_c = len({d.core_on_chip for d in col})
    except AttributeError:
        n_y, n_z, n_c = n_req, 1, 1
    if n_y * n_z * n_c != n_req:
        n_y, n_z, n_c = n_req, 1, 1
    return Mesh(np.asarray(devs).reshape(n_y, n_z, n_c, n_tp), ("ry", "rz", "rc", "tp"))


def solution(mesh):
    grid = torus_mesh(mesh)
    req = ("ry", "rz", "rc")
    in_specs = (
        P(req, "tp"),
        P(),
        P(None, None, "tp"),
        P(req, "tp", None),
        P(req, None, None, "tp"),
        P(req, None),
        P(req, None),
        P(req, None),
    )
    out_specs = P(req, "tp")
    return jax.shard_map(shards, mesh=grid, in_specs=in_specs, out_specs=out_specs, check_vma=False)
```
